512 devices in a mesh: fsdp: 8 (over z_hi, core), seq: 64 (over z_lo, x, y).
Axes of the slice: x: 4, y: 8, z: 8 (z_hi: 4, z_lo: 2; z = z_hi * 2 + z_lo), core: 2. Of those that a mesh axis runs over, the one named last changes fastest.
Arguments:
- hidden: bfloat16 [8192, 8192], P('seq', 'fsdp'), may hold values from -6 to 6
- queries: bfloat16 [8192, 8192], P('seq', 'fsdp'), may hold values from -160 to 160
- kv_weight: bfloat16 [8192, 2048], P('fsdp'), may hold values from -0.09375 to 0.09375
- kv_bias: float32 [2048], replicated, may hold values from -5 to 5
- parents: int32 [64], replicated, may hold values from 0 to 62, as said below
- slot_block: int32 [64], replicated, may hold values from 0 to 63, each once
Outputs:
- attended: bfloat16 [8192, 8192], P('seq', 'fsdp')
The draws below stay inside these ranges and needn't reach their ends.
Inputs may be any that keep to these rules, and one draw needn't show every extreme that they name: parents[0] = 0; every other block's parent has a lower number; blocks below 32 form one chain from block 0.
All inputs are finite; a program needn't handle non-finite values.
Results may differ from the reference program's by a relative error of at most 0.018.
Values may be sent and summed in bfloat16 or wider, within the bound.
No kernel may reach another device: no remote copies, remote signals or barrier semaphores. Data moves between devices by JAX's collectives and lax.ppermute only.
A program may use at most 64 MiB of HBM per device.

```python
import math
import jax
import jax.numpy as jnp
from jax import lax

D = 8192
HD = 128
GRP = 8
BLOCK = 128
QH = 64
KVH = 8
NB = 64
TREE_TOK = 8192


def draw_parents(key, part):
    block_ids = jnp.arange(NB, dtype=jnp.int32)
    first_branch = NB // 2
    stay_key, jump_key = jax.random.split(key)
    stay_flag = jax.random.randint(stay_key, (NB,), 0, 4) > 0
    stay_flag = stay_flag | (block_ids == NB - 1)
    raw_jump = jax.random.randint(jump_key, (NB,), 0, 1 << 20)
    span_size = jnp.maximum(block_ids - first_branch + 1, 1)
    jump_to = first_branch - 1 + raw_jump % span_size
    branch_parent = jnp.where(stay_flag, block_ids - 1, jump_to)
    chain_parent = jnp.maximum(block_ids - 1, 0)
    return jnp.where(block_ids < first_branch, chain_parent, branch_parent).astype(jnp.int32)


def draw_queries(key, part):
    base_key = jax.random.fold_in(key, 0)
    shape_full = (TREE_TOK, QH * HD)
    values = jax.random.truncated_normal(base_key, -6.0, 6.0, shape_full, jnp.float32)
    return values.astype(jnp.bfloat16)


def spiked(values, rng, source, target, blocks, factor):
    owner, partner = [(jnp.arange(values.shape[dim]) // (values.shape[dim] // blocks)).reshape([-1 if axis == dim else 1 for axis in range(values.ndim)]) for dim in (source, target)]
    chosen = jax.random.permutation(rng, blocks)[partner]
    strong = (owner == chosen) | (owner == (partner + blocks // 2) % blocks)
    return jnp.where(strong, factor * values, values)


def steps_of(stream_key, shape, cuts, low, top_value):
    def one(position, shards_of):
        draws = jax.random.uniform(jax.random.fold_in(jax.random.fold_in(stream_key, 6), position), (shards_of,), jnp.float32, low / len(cuts), top_value / len(cuts))
        return jnp.repeat(jnp.exp(draws), shape[position] // shards_of).reshape((-1,) + (1,) * (len(shape) - position - 1))

    factor_of = one(*cuts[0])
    for cut in cuts[1:]:
        factor_of = factor_of * one(*cut)
    return factor_of


def centred(stream_key, shape, scale, reach, cuts=(), kind=jnp.bfloat16):
    level = steps_of(stream_key, shape, cuts, -0.22, 0.18) if cuts else 1.0
    values = jax.random.normal(stream_key, shape, jnp.float32) * scale * level
    return jnp.minimum(jnp.maximum(values, -reach), reach).astype(kind)


def bell_draw_with(rng, extent, spread, limit, pieces, heavy, kind=jnp.bfloat16):
    drawn = spread * jax.random.normal(rng, extent, jnp.float32)
    if pieces:
        drawn = drawn * steps_of(rng, extent, pieces, -0.22, 0.18)
    return jnp.clip(spiked(drawn, jax.random.fold_in(rng, 3), *heavy), -limit, limit).astype(kind)


def setup_inputs(seed: int = 0) -> dict:
    keys = jax.random.split(jax.random.key(seed), 7)
    return {
        "hidden": centred(keys[0], (TREE_TOK, D), 1.0, 6.0, ((0, 64), (1, 8))),
        "queries": draw_queries(jax.random.fold_in(keys[6], 71), 0),
        "kv_weight": bell_draw_with(keys[2], (D, 2 * KVH * HD), D ** -0.5, 0.09375, ((0, 8),), (0, 1, 8, 2.0)),
        "kv_bias": centred(keys[3], (2 * KVH * HD,), 1.0, 5.0, (), jnp.float32),
        "parents": draw_parents(jax.random.fold_in(keys[6], 71), 0),
        "slot_block": jax.random.permutation(keys[5], NB).astype(jnp.int32),
    }


def ancestry_table(parents, slot_block):
    block_count = parents.shape[0]
    block_ids = jnp.arange(block_count, dtype=jnp.int32)
    linked = (parents[:, None] == block_ids[None, :]).astype(jnp.float32)
    ancestry = jnp.maximum(jnp.eye(block_count, dtype=jnp.float32), linked)
    for sweep in range(block_count.bit_length()):
        ancestry = jnp.minimum(jnp.dot(ancestry, ancestry, precision=lax.Precision.HIGHEST), 1.0)
    placement = (slot_block[:, None] == block_ids[None, :]).astype(jnp.float32)
    first_pass = jnp.dot(placement, ancestry, precision=lax.Precision.HIGHEST)
    return jnp.dot(first_pass, placement.T, precision=lax.Precision.HIGHEST)

def reference(hidden, queries, kv_weight, kv_bias, parents, slot_block):
    visible = ancestry_table(parents, slot_block)
    projected = (jnp.dot(hidden, kv_weight, preferred_element_type=jnp.float32) + kv_bias).astype(jnp.bfloat16)
    projected = projected.reshape(TREE_TOK, KVH, 2, HD)
    token_slots = jnp.arange(TREE_TOK, dtype=jnp.int32) // BLOCK
    token_offset = jnp.arange(TREE_TOK, dtype=jnp.int32) % BLOCK
    inner_offset = jnp.arange(BLOCK, dtype=jnp.int32)
    query_heads = queries.reshape(TREE_TOK, QH, HD)
    score_scale = 1.0 / math.sqrt(HD)

    def per_slot(slot):
        query_block = lax.dynamic_slice_in_dim(query_heads, slot * BLOCK, BLOCK, 0)
        slot_row = jnp.take(visible, slot, axis=0)
        row_ok = jnp.take(slot_row, token_slots) > 0.5
        allowed = row_ok[None, :] & ((token_slots[None, :] != slot) | (token_offset[None, :] <= inner_offset[:, None]))

        def per_group(group):
            query_group = lax.dynamic_slice_in_dim(query_block, group * GRP, GRP, 1).astype(jnp.float32)
            key_rows = jnp.take(projected, group, axis=1)[:, 0].astype(jnp.float32)
            value_rows = jnp.take(projected, group, axis=1)[:, 1].astype(jnp.float32)
            scores = jnp.einsum('qhd,kd->qhk', query_group, key_rows) * score_scale
            masked = jnp.where(allowed[:, None, :], scores, -1e+30)
            row_max = lax.optimization_barrier(jnp.max(masked, axis=-1, keepdims=True))
            expo = jnp.where(allowed[:, None, :], jnp.exp(masked - row_max), 0.0)
            denominator = lax.optimization_barrier(jnp.sum(expo, axis=-1))
            weights = lax.optimization_barrier(expo.astype(jnp.bfloat16)).astype(jnp.float32)
            numerator = jnp.einsum('qhk,kd->qhd', weights, value_rows)
            return numerator / denominator[..., None]
        groups_out = lax.map(per_group, jnp.arange(KVH, dtype=jnp.int32))
        return groups_out.transpose(1, 0, 2, 3).reshape(BLOCK, QH * HD).astype(jnp.bfloat16)
    result = lax.map(per_slot, jnp.arange(NB, dtype=jnp.int32))
    return result.reshape(TREE_TOK, QH * HD)
```

```python
import math

import jax
import jax.numpy as jnp
import numpy as np
from jax import lax
from jax.sharding import Mesh
from jax.sharding import PartitionSpec as P

HD = 128
BLOCK = 128
FSDP_AXES = ("zh", "c")
SEQ_AXES = ("zl", "x", "y")


def ancestry_table(parents, slot_block):
    block_count = parents.shape[0]
    block_ids = jnp.arange(block_count, dtype=jnp.int32)
    linked = (parents[:, None] == block_ids[None, :]).astype(jnp.float32)
    ancestry = jnp.maximum(jnp.eye(block_count, dtype=jnp.float32), linked)
    for sweep in range(block_count.bit_length()):
        ancestry = jnp.minimum(jnp.dot(ancestry, ancestry, precision=lax.Precision.HIGHEST), 1.0)
    placement = (slot_block[:, None] == block_ids[None, :]).astype(jnp.float32)
    first_pass = jnp.dot(placement, ancestry, precision=lax.Precision.HIGHEST)
    return jnp.dot(first_pass, placement.T, precision=lax.Precision.HIGHEST)


def keep_state(state_now):
    return state_now


def seq_index():
    return (lax.axis_index("zl") * lax.axis_size("x") + lax.axis_index("x")) * lax.axis_size("y") + lax.axis_index("y")


def fsdp_index():
    return lax.axis_index("zh") * lax.axis_size("c") + lax.axis_index("c")


def shards(hidden, queries, kv_weight, kv_bias, parents, slot_block):
    tok_rows = hidden.shape[0]
    per_device = tok_rows // BLOCK
    head_count = queries.shape[1] // HD
    score_scale = 1.0 / math.sqrt(HD)
    f_index = fsdp_index()
    n_zh = lax.axis_size("zh")
    n_c = lax.axis_size("c")
    partial_sums = jnp.dot(hidden, kv_weight, preferred_element_type=jnp.float32)
    cols = partial_sums.shape[1]
    per_head = cols // (n_zh * n_c)
    regrouped = partial_sums.reshape(tok_rows, n_zh, n_c, per_head).transpose(0, 2, 1, 3).reshape(tok_rows, cols)
    half = lax.psum_scatter(regrouped, "c", scatter_dimension=1, tiled=True)
    head_cols = lax.psum_scatter(half, "zh", scatter_dimension=1, tiled=True)
    head_bias = lax.dynamic_slice_in_dim(kv_bias, f_index * 2 * HD, 2 * HD, 0)
    both_parts = (head_cols + head_bias).astype(jnp.bfloat16)
    visible = ancestry_table(parents, slot_block)
    first_slot = seq_index() * per_device
    own_visible = lax.dynamic_slice_in_dim(visible, first_slot, per_device, 0)
    row_slot = first_slot + jnp.arange(tok_rows, dtype=jnp.int32) // BLOCK
    row_offset = jnp.arange(tok_rows, dtype=jnp.int32) % BLOCK
    query_heads = queries.reshape(tok_rows, head_count, HD)
    initial = (
        jnp.full((tok_rows, head_count), -1e30, jnp.float32),
        jnp.zeros((tok_rows, head_count), jnp.float32),
        jnp.zeros((tok_rows, head_count, HD), jnp.float32),
    )
    gathered = lax.all_gather(both_parts, "zl", axis=0, tiled=True)
    gathered = lax.all_gather(gathered, "y", axis=0, tiled=True)
    gathered = lax.all_gather(gathered, "x", axis=0, tiled=True)
    n_zl, n_x, n_y = lax.axis_size("zl"), lax.axis_size("x"), lax.axis_size("y")
    gathered = gathered.reshape(n_x, n_y, n_zl, tok_rows, 2 * HD).transpose(2, 0, 1, 3, 4).reshape(-1, 2 * HD)
    key_piece = gathered[:, :HD]
    value_piece = gathered[:, HD:]
    piece_blocks = key_piece.shape[0] // BLOCK
    group = math.gcd(piece_blocks, 8)
    tile = group * BLOCK
    tile_count = piece_blocks // group
    key_offset = jnp.arange(tile, dtype=jnp.int32) % BLOCK
    key_inner = jnp.arange(tile, dtype=jnp.int32) // BLOCK

    def one_tile(tile_index, state_now):
        key_slot_first = tile_index * group
        tile_visible = lax.dynamic_slice_in_dim(own_visible, key_slot_first, group, 1)

        def attend(state_in):
            running_max, running_sum, numerator = state_in
            key_tile = lax.dynamic_slice_in_dim(key_piece, tile_index * tile, tile, 0)
            value_tile = lax.dynamic_slice_in_dim(value_piece, tile_index * tile, tile, 0)
            scores = (
                jnp.einsum("qhd,kd->qhk", query_heads, key_tile, preferred_element_type=jnp.float32)
                * score_scale
            )
            spread = jnp.repeat(jnp.repeat(tile_visible, BLOCK, axis=0), BLOCK, axis=1) > 0.5
            key_slot = key_slot_first + key_inner
            allowed = spread & (
                (row_slot[:, None] != key_slot[None, :])
                | (key_offset[None, :] <= row_offset[:, None])
            )
            masked = jnp.where(allowed[:, None, :], scores, -1e30)
            new_max = jnp.maximum(running_max, jnp.max(masked, axis=-1))
            expo = jnp.where(allowed[:, None, :], jnp.exp(masked - new_max[..., None]), 0.0)
            factor = jnp.exp(running_max - new_max)
            new_sum = running_sum * factor + jnp.sum(expo, axis=-1)
            update = jnp.einsum(
                "qhk,kd->qhd",
                expo.astype(jnp.bfloat16),
                value_tile,
                preferred_element_type=jnp.float32,
            )
            new_numerator = numerator * factor[..., None] + update
            return (new_max, new_sum, new_numerator)

        return lax.cond(jnp.max(tile_visible) > 0.5, attend, keep_state, state_now)

    final_max, final_sum, final_numerator = lax.fori_loop(0, tile_count, one_tile, initial)
    attended = final_numerator / final_sum[..., None]
    return attended.reshape(tok_rows, head_count * HD).astype(jnp.bfloat16)


def solution(mesh):
    n_fsdp, n_seq = mesh.devices.shape
    n_c = 2
    n_zh = n_fsdp // n_c
    n_zl = 2
    n_y = 8
    n_x = n_seq // (n_zl * n_y)
    fine = Mesh(mesh.devices.reshape(n_zh, n_c, n_zl, n_x, n_y), FSDP_AXES + SEQ_AXES)
    tok = P(SEQ_AXES, FSDP_AXES)
    return jax.shard_map(
        shards,
        mesh=fine,
        in_specs=(tok, tok, P(FSDP_AXES, None), P(), P(), P()),
        out_specs=tok,
        check_vma=False,
    )
```

```python
import math

import jax
import jax.numpy as jnp
import numpy as np
from jax import lax
from jax.experimental import pallas as pl
from jax.experimental.pallas import tpu as pltpu
from jax.sharding import Mesh
from jax.sharding import PartitionSpec as P

HD = 128
BLOCK = 128
FSDP_AXES = ("zh", "c")
SEQ_AXES = ("zl", "x", "y")


def ancestry_table(parents, slot_block):
    block_count = parents.shape[0]
    block_ids = jnp.arange(block_count, dtype=jnp.int32)
    linked = (parents[:, None] == block_ids[None, :]).astype(jnp.float32)
    ancestry = jnp.maximum(jnp.eye(block_count, dtype=jnp.float32), linked)
    for sweep in range(block_count.bit_length()):
        ancestry = jnp.minimum(jnp.dot(ancestry, ancestry, precision=lax.Precision.HIGHEST), 1.0)
    placement = (slot_block[:, None] == block_ids[None, :]).astype(jnp.float32)
    first_pass = jnp.dot(placement, ancestry, precision=lax.Precision.HIGHEST)
    return jnp.dot(first_pass, placement.T, precision=lax.Precision.HIGHEST)


def seq_index():
    return (lax.axis_index("zl") * lax.axis_size("x") + lax.axis_index("x")) * lax.axis_size("y") + lax.axis_index("y")


def fsdp_index():
    return lax.axis_index("zh") * lax.axis_size("c") + lax.axis_index("c")


def shards(hidden, queries, kv_weight, kv_bias, parents, slot_block):
    tok_rows = hidden.shape[0]
    per_device = tok_rows // BLOCK
    head_count = queries.shape[1] // HD
    score_scale = 1.0 / math.sqrt(HD)
    f_index = fsdp_index()
    n_zh = lax.axis_size("zh")
    n_c = lax.axis_size("c")
    partial_sums = jnp.dot(hidden, kv_weight, preferred_element_type=jnp.float32)
    cols = partial_sums.shape[1]
    per_head = cols // (n_zh * n_c)
    regrouped = partial_sums.reshape(tok_rows, n_zh, n_c, per_head).transpose(0, 2, 1, 3).reshape(tok_rows, cols)
    half = lax.psum_scatter(regrouped, "c", scatter_dimension=1, tiled=True)
    head_cols = lax.psum_scatter(half, "zh", scatter_dimension=1, tiled=True)
    head_bias = lax.dynamic_slice_in_dim(kv_bias, f_index * 2 * HD, 2 * HD, 0)
    both_parts = (head_cols + head_bias).astype(jnp.bfloat16)
    visible = ancestry_table(parents, slot_block)
    first_slot = seq_index() * per_device
    own_visible = lax.dynamic_slice_in_dim(visible, first_slot, per_device, 0)
    gathered = lax.all_gather(both_parts, "zl", axis=0, tiled=True)
    gathered = lax.all_gather(gathered, "y", axis=0, tiled=True)
    gathered = lax.all_gather(gathered, "x", axis=0, tiled=True)
    n_zl, n_x, n_y = lax.axis_size("zl"), lax.axis_size("x"), lax.axis_size("y")
    own_slot = first_slot
    slots = jnp.arange(visible.shape[1], dtype=jnp.int32)
    slot_zl = slots // (n_x * n_y)
    slot_x = (slots // n_y) % n_x
    slot_y = slots % n_y
    physical = (slot_x * n_y + slot_y) * n_zl + slot_zl
    seen = own_visible[0] > 0.5
    count = jnp.sum(seen.astype(jnp.int32))
    position = jnp.cumsum(seen.astype(jnp.int32)) - 1
    wanted = jnp.minimum(slots, count - 1)
    hit = seen[None, :] & (position[None, :] == wanted[:, None])
    order = jnp.sum(jnp.where(hit, slots[None, :], 0), axis=1).astype(jnp.int32)
    order_physical = physical[order]
    diagonal = (order == own_slot).astype(jnp.int32)
    return attention(order_physical, diagonal, count.reshape(1), queries, gathered, head_count, score_scale)


def attention(order_physical, diagonal, count, queries, kv, head_count, score_scale):
    tok_rows = queries.shape[0]
    rows = tok_rows * head_count
    steps = order_physical.shape[0]

    def kernel(order_ref, diag_ref, count_ref, q_ref, kv_ref, o_ref, q_scr, m_scr, l_scr, acc_scr):
        i = pl.program_id(0)

        @pl.when(i == 0)
        def _():
            for h in range(head_count):
                q_scr[h * tok_rows:(h + 1) * tok_rows, :] = q_ref[:, h * HD:(h + 1) * HD]
            m_scr[...] = jnp.full(m_scr.shape, -1e30, jnp.float32)
            l_scr[...] = jnp.zeros(l_scr.shape, jnp.float32)
            acc_scr[...] = jnp.zeros(acc_scr.shape, jnp.float32)

        @pl.when(i < count_ref[0])
        def _():
            kv_blk = kv_ref[...]
            k_blk = kv_blk[:, :HD]
            v_blk = kv_blk[:, HD:]
            scores = lax.dot_general(
                q_scr[...], k_blk, (((1,), (1,)), ((), ())), preferred_element_type=jnp.float32
            ) * score_scale
            tok = lax.broadcasted_iota(jnp.int32, (rows, BLOCK), 0) % tok_rows
            key = lax.broadcasted_iota(jnp.int32, (rows, BLOCK), 1)
            allowed = (key <= tok) | (diag_ref[i] == 0)
            scores = jnp.where(allowed, scores, -1e30)
            m_old = m_scr[...]
            m_new = jnp.maximum(m_old, jnp.max(scores, axis=1, keepdims=True))
            expo = jnp.exp(scores - m_new)
            factor = jnp.exp(m_old - m_new)
            l_scr[...] = l_scr[...] * factor + jnp.sum(expo, axis=1, keepdims=True)
            acc_scr[...] = acc_scr[...] * factor + jnp.dot(
                expo.astype(jnp.bfloat16), v_blk, preferred_element_type=jnp.float32
            )
            m_scr[...] = m_new

        @pl.when(i == steps - 1)
        def _():
            result = acc_scr[...] / l_scr[...]
            for h in range(head_count):
                o_ref[:, h * HD:(h + 1) * HD] = result[h * tok_rows:(h + 1) * tok_rows].astype(o_ref.dtype)

    grid_spec = pltpu.PrefetchScalarGridSpec(
        num_scalar_prefetch=3,
        grid=(steps,),
        in_specs=[
            pl.BlockSpec((tok_rows, head_count * HD), lambda i, o, d, c: (0, 0)),
            pl.BlockSpec((BLOCK, 2 * HD), lambda i, o, d, c: (o[i], 0)),
        ],
        out_specs=pl.BlockSpec((tok_rows, head_count * HD), lambda i, o, d, c: (0, 0)),
        scratch_shapes=[
            pltpu.VMEM((rows, HD), jnp.bfloat16),
            pltpu.VMEM((rows, 1), jnp.float32),
            pltpu.VMEM((rows, 1), jnp.float32),
            pltpu.VMEM((rows, HD), jnp.float32),
        ],
    )
    return pl.pallas_call(
        kernel,
        grid_spec=grid_spec,
        out_shape=jax.ShapeDtypeStruct((tok_rows, head_count * HD), jnp.bfloat16),
        compiler_params=pltpu.CompilerParams(dimension_semantics=("arbitrary",)),
    )(order_physical, diagonal, count, queries, kv)


def solution(mesh):
    n_fsdp, n_seq = mesh.devices.shape
    n_c = 2
    n_zh = n_fsdp // n_c
    n_zl = 2
    n_y = 8
    n_x = n_seq // (n_zl * n_y)
    fine = Mesh(mesh.devices.reshape(n_zh, n_c, n_zl, n_x, n_y), FSDP_AXES + SEQ_AXES)
    tok = P(SEQ_AXES, FSDP_AXES)
    return jax.shard_map(
        shards,
        mesh=fine,
        in_specs=(tok, tok, P(FSDP_AXES, None), P(), P(), P()),
        out_specs=tok,
        check_vma=False,
    )
```

```python
import math

import jax
import jax.numpy as jnp
import numpy as np
from jax import lax
from jax.experimental import pallas as pl
from jax.experimental.pallas import tpu as pltpu
from jax.sharding import Mesh
from jax.sharding import PartitionSpec as P

HD = 128
BLOCK = 128
FSDP_AXES = ("zh", "c")
SEQ_AXES = ("zl", "x", "y")


def ancestry_table(parents, slot_block):
    block_count = parents.shape[0]
    block_ids = jnp.arange(block_count, dtype=jnp.int32)
    linked = (parents[:, None] == block_ids[None, :]).astype(jnp.float32)
    ancestry = jnp.maximum(jnp.eye(block_count, dtype=jnp.float32), linked)
    for sweep in range(block_count.bit_length()):
        ancestry = jnp.minimum(jnp.dot(ancestry, ancestry, precision=lax.Precision.HIGHEST), 1.0)
    placement = (slot_block[:, None] == block_ids[None, :]).astype(jnp.float32)
    first_pass = jnp.dot(placement, ancestry, precision=lax.Precision.HIGHEST)
    return jnp.dot(first_pass, placement.T, precision=lax.Precision.HIGHEST)


def seq_index():
    return (lax.axis_index("zl") * lax.axis_size("x") + lax.axis_index("x")) * lax.axis_size("y") + lax.axis_index("y")


def fsdp_index():
    return lax.axis_index("zh") * lax.axis_size("c") + lax.axis_index("c")


def shards(hidden, queries, kv_weight, kv_bias, parents, slot_block):
    tok_rows = hidden.shape[0]
    per_device = tok_rows // BLOCK
    head_count = queries.shape[1] // HD
    score_scale = 1.0 / math.sqrt(HD)
    f_index = fsdp_index()
    n_zh = lax.axis_size("zh")
    n_c = lax.axis_size("c")
    partial_sums = jnp.dot(hidden, kv_weight, preferred_element_type=jnp.float32)
    cols = partial_sums.shape[1]
    per_head = cols // (n_zh * n_c)
    regrouped = partial_sums.reshape(tok_rows, n_zh, n_c, per_head).transpose(0, 2, 1, 3).reshape(tok_rows, cols)
    half = lax.psum_scatter(regrouped, "c", scatter_dimension=1, tiled=True)
    head_cols = lax.psum_scatter(half, "zh", scatter_dimension=1, tiled=True)
    head_bias = lax.dynamic_slice_in_dim(kv_bias, f_index * 2 * HD, 2 * HD, 0)
    both_parts = (head_cols + head_bias).astype(jnp.bfloat16)
    kv_block = jnp.concatenate([both_parts[:, :HD], both_parts[:, HD:].T], axis=0)
    visible = ancestry_table(parents, slot_block)
    own_slot = seq_index() * per_device
    own_visible = lax.dynamic_slice_in_dim(visible, own_slot, per_device, 0)
    gathered = lax.all_gather(kv_block, "zl", axis=0, tiled=True)
    gathered = lax.all_gather(gathered, "y", axis=0, tiled=True)
    gathered = lax.all_gather(gathered, "x", axis=0, tiled=True)
    n_zl, n_x, n_y = lax.axis_size("zl"), lax.axis_size("x"), lax.axis_size("y")
    slots = jnp.arange(visible.shape[1], dtype=jnp.int32)
    slot_zl = slots // (n_x * n_y)
    slot_x = (slots // n_y) % n_x
    slot_y = slots % n_y
    physical = (slot_x * n_y + slot_y) * n_zl + slot_zl
    others = (own_visible[0] > 0.5) & (slots != own_slot)
    count = jnp.sum(others.astype(jnp.int32)) + 1
    position = jnp.cumsum(others.astype(jnp.int32))
    wanted = jnp.minimum(slots, count - 1)
    hit = others[None, :] & (position[None, :] == wanted[:, None])
    order = jnp.where(wanted == 0, own_slot, jnp.sum(jnp.where(hit, slots[None, :], 0), axis=1))
    order_physical = physical[order].astype(jnp.int32)
    return attention(order_physical, count.reshape(1), queries, gathered, head_count, score_scale)


def attention(order_physical, count, queries, kv, head_count, score_scale):
    tok_rows = queries.shape[0]
    rows = tok_rows * head_count
    steps = order_physical.shape[0] // 2

    def kernel(order_ref, count_ref, q_ref, kva_ref, kvb_ref, o_ref, q_scr, m_scr, l_scr, acc_scr):
        i = pl.program_id(0)

        @pl.when(i == 0)
        def _():
            for h in range(head_count):
                q_h = q_ref[:, h * HD:(h + 1) * HD].astype(jnp.float32)
                q_scr[:, h * tok_rows:(h + 1) * tok_rows] = q_h.T.astype(jnp.bfloat16)
            m_scr[...] = jnp.full(m_scr.shape, -1e30, jnp.float32)
            l_scr[...] = jnp.zeros(l_scr.shape, jnp.float32)
            acc_scr[...] = jnp.zeros(acc_scr.shape, jnp.float32)

        def scores_of(kv_ref, causal):
            s_t = jnp.dot(kv_ref[:BLOCK, :], q_scr[...], preferred_element_type=jnp.float32) * score_scale
            if causal:
                key = lax.broadcasted_iota(jnp.int32, (BLOCK, rows), 0)
                tok = lax.broadcasted_iota(jnp.int32, (BLOCK, rows), 1) % tok_rows
                s_t = jnp.where(key <= tok, s_t, -1e30)
            return s_t

        def step(first_causal, with_second):
            parts = [(scores_of(kva_ref, first_causal), kva_ref)]
            if with_second:
                parts.append((scores_of(kvb_ref, False), kvb_ref))
            m_old = m_scr[...]
            m_new = m_old
            for s_t, _ in parts:
                m_new = jnp.maximum(m_new, jnp.max(s_t, axis=0, keepdims=True))
            factor = jnp.exp(m_old - m_new)
            l_new = l_scr[...] * factor
            acc_new = acc_scr[...] * factor
            for s_t, ref in parts:
                expo = jnp.exp(s_t - m_new)
                l_new = l_new + jnp.sum(expo, axis=0, keepdims=True)
                acc_new = acc_new + jnp.dot(ref[BLOCK:, :], expo.astype(jnp.bfloat16), preferred_element_type=jnp.float32)
            l_scr[...] = l_new
            acc_scr[...] = acc_new
            m_scr[...] = m_new

        n = count_ref[0]
        second = 2 * i + 1 < n

        @pl.when((i == 0) & second)
        def _():
            step(True, True)

        @pl.when((i == 0) & jnp.logical_not(second))
        def _():
            step(True, False)

        @pl.when((i > 0) & second)
        def _():
            step(False, True)

        @pl.when((i > 0) & (2 * i < n) & jnp.logical_not(second))
        def _():
            step(False, False)

        @pl.when(i == steps - 1)
        def _():
            for h in range(head_count):
                cols = slice(h * tok_rows, (h + 1) * tok_rows)
                result = acc_scr[:, cols] / l_scr[:, cols]
                o_ref[:, h * HD:(h + 1) * HD] = result.T.astype(o_ref.dtype)

    grid_spec = pltpu.PrefetchScalarGridSpec(
        num_scalar_prefetch=2,
        grid=(steps,),
        in_specs=[
            pl.BlockSpec((tok_rows, head_count * HD), lambda i, o, c: (0, 0)),
            pl.BlockSpec((2 * BLOCK, HD), lambda i, o, c: (o[2 * i], 0)),
            pl.BlockSpec((2 * BLOCK, HD), lambda i, o, c: (o[2 * i + 1], 0)),
        ],
        out_specs=pl.BlockSpec((tok_rows, head_count * HD), lambda i, o, c: (0, 0)),
        scratch_shapes=[
            pltpu.VMEM((HD, rows), jnp.bfloat16),
            pltpu.VMEM((1, rows), jnp.float32),
            pltpu.VMEM((1, rows), jnp.float32),
            pltpu.VMEM((HD, rows), jnp.float32),
        ],
    )
    return pl.pallas_call(
        kernel,
        grid_spec=grid_spec,
        out_shape=jax.ShapeDtypeStruct((tok_rows, head_count * HD), jnp.bfloat16),
        compiler_params=pltpu.CompilerParams(dimension_semantics=("arbitrary",)),
    )(order_physical, count, queries, kv, kv)


def solution(mesh):
    n_fsdp, n_seq = mesh.devices.shape
    n_c = 2
    n_zh = n_fsdp // n_c
    n_zl = 2
    n_y = 8
    n_x = n_seq // (n_zl * n_y)
    fine = Mesh(mesh.devices.reshape(n_zh, n_c, n_zl, n_x, n_y), FSDP_AXES + SEQ_AXES)
    tok = P(SEQ_AXES, FSDP_AXES)
    return jax.shard_map(
        shards,
        mesh=fine,
        in_specs=(tok, tok, P(FSDP_AXES, None), P(), P(), P()),
        out_specs=tok,
        check_vma=False,
    )
```

```python
import math

import jax
import jax.numpy as jnp
import numpy as np
from jax import lax
from jax.experimental import pallas as pl
from jax.experimental.pallas import tpu as pltpu
from jax.sharding import Mesh
from jax.sharding import PartitionSpec as P

HD = 128
BLOCK = 128
FSDP_AXES = ("zh", "c")
SEQ_AXES = ("zl", "x", "y")


def ancestry_table(parents, slot_block):
    block_count = parents.shape[0]
    block_ids = jnp.arange(block_count, dtype=jnp.int32)
    linked = (parents[:, None] == block_ids[None, :]).astype(jnp.float32)
    ancestry = jnp.maximum(jnp.eye(block_count, dtype=jnp.float32), linked)
    for sweep in range(block_count.bit_length()):
        ancestry = jnp.minimum(jnp.dot(ancestry, ancestry, precision=lax.Precision.HIGHEST), 1.0)
    placement = (slot_block[:, None] == block_ids[None, :]).astype(jnp.float32)
    first_pass = jnp.dot(placement, ancestry, precision=lax.Precision.HIGHEST)
    return jnp.dot(first_pass, placement.T, precision=lax.Precision.HIGHEST)


def seq_index():
    return (lax.axis_index("zl") * lax.axis_size("x") + lax.axis_index("x")) * lax.axis_size("y") + lax.axis_index("y")


def fsdp_index():
    return lax.axis_index("zh") * lax.axis_size("c") + lax.axis_index("c")


def shards(hidden, queries, kv_weight, kv_bias, parents, slot_block):
    tok_rows = hidden.shape[0]
    per_device = tok_rows // BLOCK
    head_count = queries.shape[1] // HD
    score_scale = 1.0 / math.sqrt(HD)
    f_index = fsdp_index()
    n_zh = lax.axis_size("zh")
    n_c = lax.axis_size("c")
    partial_sums = jnp.dot(hidden, kv_weight, preferred_element_type=jnp.float32)
    cols = partial_sums.shape[1]
    per_head = cols // (n_zh * n_c)
    regrouped = partial_sums.reshape(tok_rows, n_zh, n_c, per_head).transpose(0, 2, 1, 3).reshape(tok_rows, cols)
    half = lax.psum_scatter(regrouped, "c", scatter_dimension=1, tiled=True)
    head_cols = lax.psum_scatter(half, "zh", scatter_dimension=1, tiled=True)
    head_bias = lax.dynamic_slice_in_dim(kv_bias, f_index * 2 * HD, 2 * HD, 0)
    both_parts = (head_cols + head_bias).astype(jnp.bfloat16)
    kv_block = jnp.concatenate([both_parts[:, :HD], both_parts[:, HD:].T], axis=0)
    visible = ancestry_table(parents, slot_block)
    own_slot = seq_index() * per_device
    own_visible = lax.dynamic_slice_in_dim(visible, own_slot, per_device, 0)
    gathered = lax.all_gather(kv_block, "zl", axis=0, tiled=True)
    gathered = lax.all_gather(gathered, ("x", "y"), axis=0, tiled=True)
    n_zl, n_x, n_y = lax.axis_size("zl"), lax.axis_size("x"), lax.axis_size("y")
    slots = jnp.arange(visible.shape[1], dtype=jnp.int32)
    slot_zl = slots // (n_x * n_y)
    slot_x = (slots // n_y) % n_x
    slot_y = slots % n_y
    physical = (slot_x * n_y + slot_y) * n_zl + slot_zl
    others = (own_visible[0] > 0.5) & (slots != own_slot)
    count = jnp.sum(others.astype(jnp.int32)) + 1
    position = jnp.cumsum(others.astype(jnp.int32))
    wanted = jnp.minimum(slots, count - 1)
    hit = others[None, :] & (position[None, :] == wanted[:, None])
    order = jnp.where(wanted == 0, own_slot, jnp.sum(jnp.where(hit, slots[None, :], 0), axis=1))
    order_physical = physical[order].astype(jnp.int32)
    return attention(order_physical, count.reshape(1), queries, gathered, head_count, score_scale)


def attention(order_physical, count, queries, kv, head_count, score_scale):
    tok_rows = queries.shape[0]
    rows = tok_rows * head_count
    steps = order_physical.shape[0] // 2

    def kernel(order_ref, count_ref, q_ref, kva_ref, kvb_ref, o_ref, q_scr, m_scr, l_scr, acc_scr):
        i = pl.program_id(0)

        @pl.when(i == 0)
        def _():
            for h in range(head_count):
                q_h = q_ref[:, h * HD:(h + 1) * HD].astype(jnp.float32)
                q_scr[:, h * tok_rows:(h + 1) * tok_rows] = q_h.T.astype(jnp.bfloat16)
            m_scr[...] = jnp.full(m_scr.shape, -1e30, jnp.float32)
            l_scr[...] = jnp.zeros(l_scr.shape, jnp.float32)
            acc_scr[...] = jnp.zeros(acc_scr.shape, jnp.float32)

        def scores_of(kv_ref, causal):
            s_t = jnp.dot(kv_ref[:BLOCK, :], q_scr[...], preferred_element_type=jnp.float32) * score_scale
            if causal:
                key = lax.broadcasted_iota(jnp.int32, (BLOCK, rows), 0)
                tok = lax.broadcasted_iota(jnp.int32, (BLOCK, rows), 1) % tok_rows
                s_t = jnp.where(key <= tok, s_t, -1e30)
            return s_t

        def step(first_causal, with_second):
            parts = [(scores_of(kva_ref, first_causal), kva_ref)]
            if with_second:
                parts.append((scores_of(kvb_ref, False), kvb_ref))
            m_old = m_scr[...]
            m_new = m_old
            for s_t, _ in parts:
                m_new = jnp.maximum(m_new, jnp.max(s_t, axis=0, keepdims=True))
            factor = jnp.exp(m_old - m_new)
            l_new = l_scr[...] * factor
            acc_new = acc_scr[...] * factor
            for s_t, ref in parts:
                expo = jnp.exp(s_t - m_new)
                l_new = l_new + jnp.sum(expo, axis=0, keepdims=True)
                acc_new = acc_new + jnp.dot(ref[BLOCK:, :], expo.astype(jnp.bfloat16), preferred_element_type=jnp.float32)
            l_scr[...] = l_new
            acc_scr[...] = acc_new
            m_scr[...] = m_new

        n = count_ref[0]
        second = 2 * i + 1 < n

        @pl.when((i == 0) & second)
        def _():
            step(True, True)

        @pl.when((i == 0) & jnp.logical_not(second))
        def _():
            step(True, False)

        @pl.when((i > 0) & second)
        def _():
            step(False, True)

        @pl.when((i > 0) & (2 * i < n) & jnp.logical_not(second))
        def _():
            step(False, False)

        @pl.when(i == steps - 1)
        def _():
            for h in range(head_count):
                cols = slice(h * tok_rows, (h + 1) * tok_rows)
                result = acc_scr[:, cols] / l_scr[:, cols]
                o_ref[:, h * HD:(h + 1) * HD] = result.T.astype(o_ref.dtype)

    grid_spec = pltpu.PrefetchScalarGridSpec(
        num_scalar_prefetch=2,
        grid=(steps,),
        in_specs=[
            pl.BlockSpec((tok_rows, head_count * HD), lambda i, o, c: (0, 0)),
            pl.BlockSpec((2 * BLOCK, HD), lambda i, o, c: (o[2 * i], 0)),
            pl.BlockSpec((2 * BLOCK, HD), lambda i, o, c: (o[2 * i + 1], 0)),
        ],
        out_specs=pl.BlockSpec((tok_rows, head_count * HD), lambda i, o, c: (0, 0)),
        scratch_shapes=[
            pltpu.VMEM((HD, rows), jnp.bfloat16),
            pltpu.VMEM((1, rows), jnp.float32),
            pltpu.VMEM((1, rows), jnp.float32),
            pltpu.VMEM((HD, rows), jnp.float32),
        ],
    )
    return pl.pallas_call(
        kernel,
        grid_spec=grid_spec,
        out_shape=jax.ShapeDtypeStruct((tok_rows, head_count * HD), jnp.bfloat16),
        compiler_params=pltpu.CompilerParams(dimension_semantics=("arbitrary",)),
    )(order_physical, count, queries, kv, kv)


def solution(mesh):
    n_fsdp, n_seq = mesh.devices.shape
    n_c = 2
    n_zh = n_fsdp // n_c
    n_zl = 2
    n_y = 8
    n_x = n_seq // (n_zl * n_y)
    fine = Mesh(mesh.devices.reshape(n_zh, n_c, n_zl, n_x, n_y), FSDP_AXES + SEQ_AXES)
    tok = P(SEQ_AXES, FSDP_AXES)
    return jax.shard_map(
        shards,
        mesh=fine,
        in_specs=(tok, tok, P(FSDP_AXES, None), P(), P(), P()),
        out_specs=tok,
        check_vma=False,
    )
```

```python
import math

import jax
import jax.numpy as jnp
import numpy as np
from jax import lax
from jax.experimental import pallas as pl
from jax.experimental.pallas import tpu as pltpu
from jax.sharding import Mesh
from jax.sharding import PartitionSpec as P

HD = 128
BLOCK = 128
FSDP_AXES = ("zh", "c")
SEQ_AXES = ("zl", "x", "y")


def ancestry_table(parents, slot_block):
    block_count = parents.shape[0]
    block_ids = jnp.arange(block_count, dtype=jnp.int32)
    linked = (parents[:, None] == block_ids[None, :]).astype(jnp.float32)
    ancestry = jnp.maximum(jnp.eye(block_count, dtype=jnp.float32), linked)
    for sweep in range(block_count.bit_length()):
        ancestry = jnp.minimum(jnp.dot(ancestry, ancestry, precision=lax.Precision.HIGHEST), 1.0)
    placement = (slot_block[:, None] == block_ids[None, :]).astype(jnp.float32)
    first_pass = jnp.dot(placement, ancestry, precision=lax.Precision.HIGHEST)
    return jnp.dot(first_pass, placement.T, precision=lax.Precision.HIGHEST)


def seq_index():
    return (lax.axis_index("zl") * lax.axis_size("x") + lax.axis_index("x")) * lax.axis_size("y") + lax.axis_index("y")


def fsdp_index():
    return lax.axis_index("zh") * lax.axis_size("c") + lax.axis_index("c")


def shards(hidden, queries, kv_weight, kv_bias, parents, slot_block):
    tok_rows = hidden.shape[0]
    per_device = tok_rows // BLOCK
    head_count = queries.shape[1] // HD
    score_scale = 1.0 / math.sqrt(HD)
    f_index = fsdp_index()
    n_zh = lax.axis_size("zh")
    n_c = lax.axis_size("c")
    cols = kv_weight.shape[1]
    per_head = cols // (n_zh * n_c)
    partial_sums = jnp.dot(hidden, kv_weight, preferred_element_type=jnp.float32)
    partial_sums = partial_sums.reshape(tok_rows, n_zh, n_c, per_head).transpose(2, 1, 0, 3)
    from_core = lax.all_to_all(partial_sums, "c", 0, 0)
    core_sums = jnp.sum(from_core, axis=0)
    from_chip = lax.all_to_all(core_sums, "zh", 0, 0)
    head_cols = jnp.sum(from_chip, axis=0)
    head_bias = lax.dynamic_slice_in_dim(kv_bias, f_index * 2 * HD, 2 * HD, 0)
    both_parts = (head_cols + head_bias).astype(jnp.bfloat16)
    kv_block = jnp.concatenate([both_parts[:, :HD], both_parts[:, HD:].T], axis=0)
    visible = ancestry_table(parents, slot_block)
    own_slot = seq_index() * per_device
    own_visible = lax.dynamic_slice_in_dim(visible, own_slot, per_device, 0)
    gathered = lax.all_gather(kv_block, "zl", axis=0, tiled=True)
    gathered = lax.all_gather(gathered, ("x", "y"), axis=0, tiled=True)
    n_zl, n_x, n_y = lax.axis_size("zl"), lax.axis_size("x"), lax.axis_size("y")
    slots = jnp.arange(visible.shape[1], dtype=jnp.int32)
    slot_zl = slots // (n_x * n_y)
    slot_x = (slots // n_y) % n_x
    slot_y = slots % n_y
    physical = (slot_x * n_y + slot_y) * n_zl + slot_zl
    others = (own_visible[0] > 0.5) & (slots != own_slot)
    count = jnp.sum(others.astype(jnp.int32)) + 1
    position = jnp.cumsum(others.astype(jnp.int32))
    wanted = jnp.minimum(slots, count - 1)
    hit = others[None, :] & (position[None, :] == wanted[:, None])
    order = jnp.where(wanted == 0, own_slot, jnp.sum(jnp.where(hit, slots[None, :], 0), axis=1))
    order_physical = physical[order].astype(jnp.int32)
    return attention(order_physical, count.reshape(1), queries, gathered, head_count, score_scale)


def attention(order_physical, count, queries, kv, head_count, score_scale):
    tok_rows = queries.shape[0]
    rows = tok_rows * head_count
    steps = order_physical.shape[0] // 2

    def kernel(order_ref, count_ref, q_ref, kva_ref, kvb_ref, o_ref, q_scr, m_scr, l_scr, acc_scr):
        i = pl.program_id(0)

        @pl.when(i == 0)
        def _():
            for h in range(head_count):
                q_h = q_ref[:, h * HD:(h + 1) * HD].astype(jnp.float32)
                q_scr[:, h * tok_rows:(h + 1) * tok_rows] = q_h.T.astype(jnp.bfloat16)
            m_scr[...] = jnp.full(m_scr.shape, -1e30, jnp.float32)
            l_scr[...] = jnp.zeros(l_scr.shape, jnp.float32)
            acc_scr[...] = jnp.zeros(acc_scr.shape, jnp.float32)

        def scores_of(kv_ref, causal):
            s_t = jnp.dot(kv_ref[:BLOCK, :], q_scr[...], preferred_element_type=jnp.float32) * score_scale
            if causal:
                key = lax.broadcasted_iota(jnp.int32, (BLOCK, rows), 0)
                tok = lax.broadcasted_iota(jnp.int32, (BLOCK, rows), 1) % tok_rows
                s_t = jnp.where(key <= tok, s_t, -1e30)
            return s_t

        def step(first_causal, with_second):
            parts = [(scores_of(kva_ref, first_causal), kva_ref)]
            if with_second:
                parts.append((scores_of(kvb_ref, False), kvb_ref))
            m_old = m_scr[...]
            m_new = m_old
            for s_t, _ in parts:
                m_new = jnp.maximum(m_new, jnp.max(s_t, axis=0, keepdims=True))
            factor = jnp.exp(m_old - m_new)
            l_new = l_scr[...] * factor
            acc_new = acc_scr[...] * factor
            for s_t, ref in parts:
                expo = jnp.exp(s_t - m_new)
                l_new = l_new + jnp.sum(expo, axis=0, keepdims=True)
                acc_new = acc_new + jnp.dot(ref[BLOCK:, :], expo.astype(jnp.bfloat16), preferred_element_type=jnp.float32)
            l_scr[...] = l_new
            acc_scr[...] = acc_new
            m_scr[...] = m_new

        n = count_ref[0]
        second = 2 * i + 1 < n

        @pl.when((i == 0) & second)
        def _():
            step(True, True)

        @pl.when((i == 0) & jnp.logical_not(second))
        def _():
            step(True, False)

        @pl.when((i > 0) & second)
        def _():
            step(False, True)

        @pl.when((i > 0) & (2 * i < n) & jnp.logical_not(second))
        def _():
            step(False, False)

        @pl.when(i == steps - 1)
        def _():
            for h in range(head_count):
                cols = slice(h * tok_rows, (h + 1) * tok_rows)
                result = acc_scr[:, cols] / l_scr[:, cols]
                o_ref[:, h * HD:(h + 1) * HD] = result.T.astype(o_ref.dtype)

    grid_spec = pltpu.PrefetchScalarGridSpec(
        num_scalar_prefetch=2,
        grid=(steps,),
        in_specs=[
            pl.BlockSpec((tok_rows, head_count * HD), lambda i, o, c: (0, 0)),
            pl.BlockSpec((2 * BLOCK, HD), lambda i, o, c: (o[2 * i], 0)),
            pl.BlockSpec((2 * BLOCK, HD), lambda i, o, c: (o[2 * i + 1], 0)),
        ],
        out_specs=pl.BlockSpec((tok_rows, head_count * HD), lambda i, o, c: (0, 0)),
        scratch_shapes=[
            pltpu.VMEM((HD, rows), jnp.bfloat16),
            pltpu.VMEM((1, rows), jnp.float32),
            pltpu.VMEM((1, rows), jnp.float32),
            pltpu.VMEM((HD, rows), jnp.float32),
        ],
    )
    return pl.pallas_call(
        kernel,
        grid_spec=grid_spec,
        out_shape=jax.ShapeDtypeStruct((tok_rows, head_count * HD), jnp.bfloat16),
        compiler_params=pltpu.CompilerParams(dimension_semantics=("arbitrary",)),
    )(order_physical, count, queries, kv, kv)


def solution(mesh):
    n_fsdp, n_seq = mesh.devices.shape
    n_c = 2
    n_zh = n_fsdp // n_c
    n_zl = 2
    n_y = 8
    n_x = n_seq // (n_zl * n_y)
    fine = Mesh(mesh.devices.reshape(n_zh, n_c, n_zl, n_x, n_y), FSDP_AXES + SEQ_AXES)
    tok = P(SEQ_AXES, FSDP_AXES)
    return jax.shard_map(
        shards,
        mesh=fine,
        in_specs=(tok, tok, P(FSDP_AXES, None), P(), P(), P()),
        out_specs=tok,
        check_vma=False,
    )
```

```python
import math

import jax
import jax.numpy as jnp
import numpy as np
from jax import lax
from jax.experimental import pallas as pl
from jax.experimental.pallas import tpu as pltpu
from jax.sharding import Mesh
from jax.sharding import PartitionSpec as P

HD = 128
BLOCK = 128
FSDP_AXES = ("zh", "c")
SEQ_AXES = ("zl", "x", "y")


def ancestry_table(parents, slot_block):
    block_count = parents.shape[0]
    block_ids = jnp.arange(block_count, dtype=jnp.int32)
    linked = (parents[:, None] == block_ids[None, :]).astype(jnp.float32)
    ancestry = jnp.maximum(jnp.eye(block_count, dtype=jnp.float32), linked)
    for sweep in range(block_count.bit_length()):
        ancestry = jnp.minimum(jnp.dot(ancestry, ancestry, precision=lax.Precision.HIGHEST), 1.0)
    placement = (slot_block[:, None] == block_ids[None, :]).astype(jnp.float32)
    first_pass = jnp.dot(placement, ancestry, precision=lax.Precision.HIGHEST)
    return jnp.dot(first_pass, placement.T, precision=lax.Precision.HIGHEST)


def seq_index():
    return (lax.axis_index("zl") * lax.axis_size("x") + lax.axis_index("x")) * lax.axis_size("y") + lax.axis_index("y")


def fsdp_index():
    return lax.axis_index("zh") * lax.axis_size("c") + lax.axis_index("c")


def shift(x, axis, n, step):
    return lax.ppermute(x, axis, [(i, (i + step) % n) for i in range(n)])


def ring_gather(x, axis, n):
    if n == 1:
        return x[None]
    ahead = [x]
    behind = [x]
    for _ in range((n - 1) // 2):
        ahead.append(shift(ahead[-1], axis, n, -1))
        behind.append(shift(behind[-1], axis, n, 1))
    middle = []
    if n % 2 == 0:
        if n == 2:
            middle = [shift(x, axis, n, 1)]
        else:
            half = x.shape[0] // 2
            far_behind = shift(behind[-1][:half], axis, n, 1)
            far_ahead = shift(ahead[-1][half:], axis, n, -1)
            middle = [jnp.concatenate([far_behind, far_ahead], axis=0)]
    return jnp.stack(ahead + middle + behind[1:][::-1], axis=0)


def shards(hidden, queries, kv_weight, kv_bias, parents, slot_block):
    tok_rows = hidden.shape[0]
    per_device = tok_rows // BLOCK
    head_count = queries.shape[1] // HD
    score_scale = 1.0 / math.sqrt(HD)
    f_index = fsdp_index()
    n_zh = lax.axis_size("zh")
    n_c = lax.axis_size("c")
    cols = kv_weight.shape[1]
    per_head = cols // (n_zh * n_c)
    partial_sums = jnp.dot(hidden, kv_weight, preferred_element_type=jnp.float32)
    partial_sums = partial_sums.reshape(tok_rows, n_zh, n_c, per_head).transpose(2, 1, 0, 3)
    from_core = lax.all_to_all(partial_sums, "c", 0, 0)
    core_sums = jnp.sum(from_core, axis=0)
    from_chip = lax.all_to_all(core_sums, "zh", 0, 0)
    head_cols = jnp.sum(from_chip, axis=0)
    head_bias = lax.dynamic_slice_in_dim(kv_bias, f_index * 2 * HD, 2 * HD, 0)
    both_parts = (head_cols + head_bias).astype(jnp.bfloat16)
    kv_block = jnp.concatenate([both_parts[:, :HD], both_parts[:, HD:].T], axis=0)
    visible = ancestry_table(parents, slot_block)
    own_slot = seq_index() * per_device
    own_visible = lax.dynamic_slice_in_dim(visible, own_slot, per_device, 0)
    n_zl, n_x, n_y = lax.axis_size("zl"), lax.axis_size("x"), lax.axis_size("y")
    pair = ring_gather(kv_block[None], "zl", n_zl)
    plane = ring_gather(pair, "y", n_y)
    gathered = ring_gather(plane, "x", n_x).reshape(-1, HD)
    slots = jnp.arange(visible.shape[1], dtype=jnp.int32)
    slot_zl = slots // (n_x * n_y)
    slot_x = (slots // n_y) % n_x
    slot_y = slots % n_y
    rel_zl = (slot_zl - lax.axis_index("zl")) % n_zl
    rel_x = (slot_x - lax.axis_index("x")) % n_x
    rel_y = (slot_y - lax.axis_index("y")) % n_y
    physical = (rel_x * n_y + rel_y) * n_zl + rel_zl
    others = (own_visible[0] > 0.5) & (slots != own_slot)
    count = jnp.sum(others.astype(jnp.int32)) + 1
    position = jnp.cumsum(others.astype(jnp.int32))
    wanted = jnp.minimum(slots, count - 1)
    hit = others[None, :] & (position[None, :] == wanted[:, None])
    order = jnp.where(wanted == 0, own_slot, jnp.sum(jnp.where(hit, slots[None, :], 0), axis=1))
    order_physical = physical[order].astype(jnp.int32)
    return attention(order_physical, count.reshape(1), queries, gathered, head_count, score_scale)


def attention(order_physical, count, queries, kv, head_count, score_scale):
    tok_rows = queries.shape[0]
    rows = tok_rows * head_count
    steps = order_physical.shape[0] // 2

    def kernel(order_ref, count_ref, q_ref, kva_ref, kvb_ref, o_ref, q_scr, m_scr, l_scr, acc_scr):
        i = pl.program_id(0)

        @pl.when(i == 0)
        def _():
            for h in range(head_count):
                q_h = q_ref[:, h * HD:(h + 1) * HD].astype(jnp.float32)
                q_scr[:, h * tok_rows:(h + 1) * tok_rows] = q_h.T.astype(jnp.bfloat16)
            m_scr[...] = jnp.full(m_scr.shape, -1e30, jnp.float32)
            l_scr[...] = jnp.zeros(l_scr.shape, jnp.float32)
            acc_scr[...] = jnp.zeros(acc_scr.shape, jnp.float32)

        def scores_of(kv_ref, causal):
            s_t = jnp.dot(kv_ref[:BLOCK, :], q_scr[...], preferred_element_type=jnp.float32) * score_scale
            if causal:
                key = lax.broadcasted_iota(jnp.int32, (BLOCK, rows), 0)
                tok = lax.broadcasted_iota(jnp.int32, (BLOCK, rows), 1) % tok_rows
                s_t = jnp.where(key <= tok, s_t, -1e30)
            return s_t

        def step(first_causal, with_second):
            parts = [(scores_of(kva_ref, first_causal), kva_ref)]
            if with_second:
                parts.append((scores_of(kvb_ref, False), kvb_ref))
            m_old = m_scr[...]
            m_new = m_old
            for s_t, _ in parts:
                m_new = jnp.maximum(m_new, jnp.max(s_t, axis=0, keepdims=True))
            factor = jnp.exp(m_old - m_new)
            l_new = l_scr[...] * factor
            acc_new = acc_scr[...] * factor
            for s_t, ref in parts:
                expo = jnp.exp(s_t - m_new)
                l_new = l_new + jnp.sum(expo, axis=0, keepdims=True)
                acc_new = acc_new + jnp.dot(ref[BLOCK:, :], expo.astype(jnp.bfloat16), preferred_element_type=jnp.float32)
            l_scr[...] = l_new
            acc_scr[...] = acc_new
            m_scr[...] = m_new

        n = count_ref[0]
        second = 2 * i + 1 < n

        @pl.when((i == 0) & second)
        def _():
            step(True, True)

        @pl.when((i == 0) & jnp.logical_not(second))
        def _():
            step(True, False)

        @pl.when((i > 0) & second)
        def _():
            step(False, True)

        @pl.when((i > 0) & (2 * i < n) & jnp.logical_not(second))
        def _():
            step(False, False)

        @pl.when(i == steps - 1)
        def _():
            for h in range(head_count):
                cols = slice(h * tok_rows, (h + 1) * tok_rows)
                result = acc_scr[:, cols] / l_scr[:, cols]
                o_ref[:, h * HD:(h + 1) * HD] = result.T.astype(o_ref.dtype)

    grid_spec = pltpu.PrefetchScalarGridSpec(
        num_scalar_prefetch=2,
        grid=(steps,),
        in_specs=[
            pl.BlockSpec((tok_rows, head_count * HD), lambda i, o, c: (0, 0)),
            pl.BlockSpec((2 * BLOCK, HD), lambda i, o, c: (o[2 * i], 0)),
            pl.BlockSpec((2 * BLOCK, HD), lambda i, o, c: (o[2 * i + 1], 0)),
        ],
        out_specs=pl.BlockSpec((tok_rows, head_count * HD), lambda i, o, c: (0, 0)),
        scratch_shapes=[
            pltpu.VMEM((HD, rows), jnp.bfloat16),
            pltpu.VMEM((1, rows), jnp.float32),
            pltpu.VMEM((1, rows), jnp.float32),
            pltpu.VMEM((HD, rows), jnp.float32),
        ],
    )
    return pl.pallas_call(
        kernel,
        grid_spec=grid_spec,
        out_shape=jax.ShapeDtypeStruct((tok_rows, head_count * HD), jnp.bfloat16),
        compiler_params=pltpu.CompilerParams(dimension_semantics=("arbitrary",)),
    )(order_physical, count, queries, kv, kv)


def solution(mesh):
    n_fsdp, n_seq = mesh.devices.shape
    n_c = 2
    n_zh = n_fsdp // n_c
    n_zl = 2
    n_y = 8
    n_x = n_seq // (n_zl * n_y)
    fine = Mesh(mesh.devices.reshape(n_zh, n_c, n_zl, n_x, n_y), FSDP_AXES + SEQ_AXES)
    tok = P(SEQ_AXES, FSDP_AXES)
    return jax.shard_map(
        shards,
        mesh=fine,
        in_specs=(tok, tok, P(FSDP_AXES, None), P(), P(), P()),
        out_specs=tok,
        check_vma=False,
    )
```

```python
import math

import jax
import jax.numpy as jnp
import numpy as np
from jax import lax
from jax.experimental import pallas as pl
from jax.experimental.pallas import tpu as pltpu
from jax.sharding import Mesh
from jax.sharding import PartitionSpec as P

HD = 128
BLOCK = 128
FSDP_AXES = ("zh", "c")
SEQ_AXES = ("zl", "x", "y")


def ancestry_table(parents, slot_block):
    block_count = parents.shape[0]
    block_ids = jnp.arange(block_count, dtype=jnp.int32)
    linked = (parents[:, None] == block_ids[None, :]).astype(jnp.float32)
    ancestry = jnp.maximum(jnp.eye(block_count, dtype=jnp.float32), linked)
    for sweep in range(block_count.bit_length()):
        ancestry = jnp.minimum(jnp.dot(ancestry, ancestry, precision=lax.Precision.HIGHEST), 1.0)
    placement = (slot_block[:, None] == block_ids[None, :]).astype(jnp.float32)
    first_pass = jnp.dot(placement, ancestry, precision=lax.Precision.HIGHEST)
    return jnp.dot(first_pass, placement.T, precision=lax.Precision.HIGHEST)


def seq_index():
    return (lax.axis_index("zl") * lax.axis_size("x") + lax.axis_index("x")) * lax.axis_size("y") + lax.axis_index("y")


def fsdp_index():
    return lax.axis_index("zh") * lax.axis_size("c") + lax.axis_index("c")


def shards(hidden, queries, kv_weight, kv_bias, parents, slot_block):
    tok_rows = hidden.shape[0]
    per_device = tok_rows // BLOCK
    head_count = queries.shape[1] // HD
    score_scale = 1.0 / math.sqrt(HD)
    f_index = fsdp_index()
    n_zh = lax.axis_size("zh")
    n_c = lax.axis_size("c")
    cols = kv_weight.shape[1]
    per_head = cols // (n_zh * n_c)
    partial_sums = jnp.dot(hidden, kv_weight, preferred_element_type=jnp.float32)
    partial_sums = partial_sums.reshape(tok_rows, n_zh, n_c, per_head).transpose(2, 1, 0, 3)
    from_core = lax.all_to_all(partial_sums, "c", 0, 0)
    core_sums = jnp.sum(from_core, axis=0)
    from_chip = lax.all_to_all(core_sums, "zh", 0, 0)
    head_cols = jnp.sum(from_chip, axis=0)
    head_bias = lax.dynamic_slice_in_dim(kv_bias, f_index * 2 * HD, 2 * HD, 0)
    both_parts = (head_cols + head_bias).astype(jnp.bfloat16)
    kv_block = jnp.concatenate([both_parts[:, :HD], both_parts[:, HD:].T], axis=0)
    visible = ancestry_table(parents, slot_block)
    own_slot = seq_index() * per_device
    own_visible = lax.dynamic_slice_in_dim(visible, own_slot, per_device, 0)
    n_zl, n_x, n_y = lax.axis_size("zl"), lax.axis_size("x"), lax.axis_size("y")
    spread = jnp.broadcast_to(kv_block[None], (n_zl * n_y,) + kv_block.shape)
    plane = lax.all_to_all(spread, ("zl", "y"), 0, 0)
    gathered = lax.all_gather(plane, "x", axis=0, tiled=True).reshape(-1, HD)
    slots = jnp.arange(visible.shape[1], dtype=jnp.int32)
    slot_zl = slots // (n_x * n_y)
    slot_x = (slots // n_y) % n_x
    slot_y = slots % n_y
    physical = (slot_x * n_zl + slot_zl) * n_y + slot_y
    others = (own_visible[0] > 0.5) & (slots != own_slot)
    count = jnp.sum(others.astype(jnp.int32)) + 1
    position = jnp.cumsum(others.astype(jnp.int32))
    wanted = jnp.minimum(slots, count - 1)
    hit = others[None, :] & (position[None, :] == wanted[:, None])
    order = jnp.where(wanted == 0, own_slot, jnp.sum(jnp.where(hit, slots[None, :], 0), axis=1))
    order_physical = physical[order].astype(jnp.int32)
    return attention(order_physical, count.reshape(1), queries, gathered, head_count, score_scale)


def attention(order_physical, count, queries, kv, head_count, score_scale):
    tok_rows = queries.shape[0]
    rows = tok_rows * head_count
    steps = order_physical.shape[0] // 2

    def kernel(order_ref, count_ref, q_ref, kva_ref, kvb_ref, o_ref, q_scr, m_scr, l_scr, acc_scr):
        i = pl.program_id(0)

        @pl.when(i == 0)
        def _():
            for h in range(head_count):
                q_h = q_ref[:, h * HD:(h + 1) * HD].astype(jnp.float32)
                q_scr[:, h * tok_rows:(h + 1) * tok_rows] = q_h.T.astype(jnp.bfloat16)
            m_scr[...] = jnp.full(m_scr.shape, -1e30, jnp.float32)
            l_scr[...] = jnp.zeros(l_scr.shape, jnp.float32)
            acc_scr[...] = jnp.zeros(acc_scr.shape, jnp.float32)

        def scores_of(kv_ref, causal):
            s_t = jnp.dot(kv_ref[:BLOCK, :], q_scr[...], preferred_element_type=jnp.float32) * score_scale
            if causal:
                key = lax.broadcasted_iota(jnp.int32, (BLOCK, rows), 0)
                tok = lax.broadcasted_iota(jnp.int32, (BLOCK, rows), 1) % tok_rows
                s_t = jnp.where(key <= tok, s_t, -1e30)
            return s_t

        def step(first_causal, with_second):
            parts = [(scores_of(kva_ref, first_causal), kva_ref)]
            if with_second:
                parts.append((scores_of(kvb_ref, False), kvb_ref))
            m_old = m_scr[...]
            m_new = m_old
            for s_t, _ in parts:
                m_new = jnp.maximum(m_new, jnp.max(s_t, axis=0, keepdims=True))
            factor = jnp.exp(m_old - m_new)
            l_new = l_scr[...] * factor
            acc_new = acc_scr[...] * factor
            for s_t, ref in parts:
                expo = jnp.exp(s_t - m_new)
                l_new = l_new + jnp.sum(expo, axis=0, keepdims=True)
                acc_new = acc_new + jnp.dot(ref[BLOCK:, :], expo.astype(jnp.bfloat16), preferred_element_type=jnp.float32)
            l_scr[...] = l_new
            acc_scr[...] = acc_new
            m_scr[...] = m_new

        n = count_ref[0]
        second = 2 * i + 1 < n

        @pl.when((i == 0) & second)
        def _():
            step(True, True)

        @pl.when((i == 0) & jnp.logical_not(second))
        def _():
            step(True, False)

        @pl.when((i > 0) & second)
        def _():
            step(False, True)

        @pl.when((i > 0) & (2 * i < n) & jnp.logical_not(second))
        def _():
            step(False, False)

        @pl.when(i == steps - 1)
        def _():
            for h in range(head_count):
                cols = slice(h * tok_rows, (h + 1) * tok_rows)
                result = acc_scr[:, cols] / l_scr[:, cols]
                o_ref[:, h * HD:(h + 1) * HD] = result.T.astype(o_ref.dtype)

    grid_spec = pltpu.PrefetchScalarGridSpec(
        num_scalar_prefetch=2,
        grid=(steps,),
        in_specs=[
            pl.BlockSpec((tok_rows, head_count * HD), lambda i, o, c: (0, 0)),
            pl.BlockSpec((2 * BLOCK, HD), lambda i, o, c: (o[2 * i], 0)),
            pl.BlockSpec((2 * BLOCK, HD), lambda i, o, c: (o[2 * i + 1], 0)),
        ],
        out_specs=pl.BlockSpec((tok_rows, head_count * HD), lambda i, o, c: (0, 0)),
        scratch_shapes=[
            pltpu.VMEM((HD, rows), jnp.bfloat16),
            pltpu.VMEM((1, rows), jnp.float32),
            pltpu.VMEM((1, rows), jnp.float32),
            pltpu.VMEM((HD, rows), jnp.float32),
        ],
    )
    return pl.pallas_call(
        kernel,
        grid_spec=grid_spec,
        out_shape=jax.ShapeDtypeStruct((tok_rows, head_count * HD), jnp.bfloat16),
        compiler_params=pltpu.CompilerParams(dimension_semantics=("arbitrary",)),
    )(order_physical, count, queries, kv, kv)


def solution(mesh):
    n_fsdp, n_seq = mesh.devices.shape
    n_c = 2
    n_zh = n_fsdp // n_c
    n_zl = 2
    n_y = 8
    n_x = n_seq // (n_zl * n_y)
    fine = Mesh(mesh.devices.reshape(n_zh, n_c, n_zl, n_x, n_y), FSDP_AXES + SEQ_AXES)
    tok = P(SEQ_AXES, FSDP_AXES)
    return jax.shard_map(
        shards,
        mesh=fine,
        in_specs=(tok, tok, P(FSDP_AXES, None), P(), P(), P()),
        out_specs=tok,
        check_vma=False,
    )
```

```python
import math

import jax
import jax.numpy as jnp
import numpy as np
from jax import lax
from jax.experimental import pallas as pl
from jax.experimental.pallas import tpu as pltpu
from jax.sharding import Mesh
from jax.sharding import PartitionSpec as P

HD = 128
BLOCK = 128
FSDP_AXES = ("zh", "c")
SEQ_AXES = ("zl", "x", "y")


def ancestry_table(parents, slot_block):
    block_count = parents.shape[0]
    block_ids = jnp.arange(block_count, dtype=jnp.int32)
    linked = (parents[:, None] == block_ids[None, :]).astype(jnp.float32)
    ancestry = jnp.maximum(jnp.eye(block_count, dtype=jnp.float32), linked)
    for sweep in range(block_count.bit_length()):
        ancestry = jnp.minimum(jnp.dot(ancestry, ancestry, precision=lax.Precision.HIGHEST), 1.0)
    placement = (slot_block[:, None] == block_ids[None, :]).astype(jnp.float32)
    first_pass = jnp.dot(placement, ancestry, precision=lax.Precision.HIGHEST)
    return jnp.dot(first_pass, placement.T, precision=lax.Precision.HIGHEST)


def seq_index():
    return (lax.axis_index("zl") * lax.axis_size("x") + lax.axis_index("x")) * lax.axis_size("y") + lax.axis_index("y")


def fsdp_index():
    return lax.axis_index("zh") * lax.axis_size("c") + lax.axis_index("c")


def shards(hidden, queries, kv_weight, kv_bias, parents, slot_block):
    tok_rows = hidden.shape[0]
    per_device = tok_rows // BLOCK
    head_count = queries.shape[1] // HD
    score_scale = 1.0 / math.sqrt(HD)
    f_index = fsdp_index()
    n_zh = lax.axis_size("zh")
    n_c = lax.axis_size("c")
    cols = kv_weight.shape[1]
    per_head = cols // (n_zh * n_c)
    partial_sums = jnp.dot(hidden, kv_weight, preferred_element_type=jnp.float32)
    partial_sums = partial_sums.reshape(tok_rows, n_zh, n_c, per_head).transpose(2, 1, 0, 3)
    from_core = lax.all_to_all(partial_sums, "c", 0, 0)
    core_sums = jnp.sum(from_core, axis=0)
    from_chip = lax.all_to_all(core_sums, "zh", 0, 0)
    head_cols = jnp.sum(from_chip, axis=0)
    head_bias = lax.dynamic_slice_in_dim(kv_bias, f_index * 2 * HD, 2 * HD, 0)
    both_parts = (head_cols + head_bias).astype(jnp.bfloat16)
    kv_block = jnp.concatenate([both_parts[:, :HD], both_parts[:, HD:].T], axis=0)
    visible = ancestry_table(parents, slot_block)
    own_slot = seq_index() * per_device
    own_visible = lax.dynamic_slice_in_dim(visible, own_slot, per_device, 0)
    n_zl, n_x, n_y = lax.axis_size("zl"), lax.axis_size("x"), lax.axis_size("y")
    plane_size = n_zl * n_y
    keys = both_parts[:, :HD]
    values_t = both_parts[:, HD:].T
    key_plane = lax.all_to_all(jnp.broadcast_to(keys[None], (plane_size,) + keys.shape), ("zl", "y"), 0, 0)
    key_all = lax.all_gather(key_plane, "x", axis=0, tiled=True).reshape(-1, HD)
    value_row = lax.all_gather(values_t[None], "x", axis=0, tiled=True)
    value_all = lax.all_to_all(
        jnp.broadcast_to(value_row[None], (plane_size,) + value_row.shape), ("zl", "y"), 0, 0
    ).reshape(-1, HD)
    slots = jnp.arange(visible.shape[1], dtype=jnp.int32)
    slot_zl = slots // (n_x * n_y)
    slot_x = (slots // n_y) % n_x
    slot_y = slots % n_y
    key_physical = (slot_x * n_zl + slot_zl) * n_y + slot_y
    value_physical = (slot_zl * n_y + slot_y) * n_x + slot_x
    others = (own_visible[0] > 0.5) & (slots != own_slot)
    count = jnp.sum(others.astype(jnp.int32)) + 1
    position = jnp.cumsum(others.astype(jnp.int32))
    wanted = jnp.minimum(slots, count - 1)
    hit = others[None, :] & (position[None, :] == wanted[:, None])
    order = jnp.where(wanted == 0, own_slot, jnp.sum(jnp.where(hit, slots[None, :], 0), axis=1))
    order_physical = jnp.stack([key_physical[order], value_physical[order]]).astype(jnp.int32)
    return attention(order_physical, count.reshape(1), queries, key_all, value_all, head_count, score_scale)


def attention(order_physical, count, queries, key_all, value_all, head_count, score_scale):
    tok_rows = queries.shape[0]
    rows = tok_rows * head_count
    steps = order_physical.shape[1] // 2

    def kernel(order_ref, count_ref, q_ref, ka_ref, kb_ref, va_ref, vb_ref, o_ref, q_scr, m_scr, l_scr, acc_scr):
        i = pl.program_id(0)

        @pl.when(i == 0)
        def _():
            for h in range(head_count):
                q_h = q_ref[:, h * HD:(h + 1) * HD].astype(jnp.float32)
                q_scr[:, h * tok_rows:(h + 1) * tok_rows] = q_h.T.astype(jnp.bfloat16)
            m_scr[...] = jnp.full(m_scr.shape, -1e30, jnp.float32)
            l_scr[...] = jnp.zeros(l_scr.shape, jnp.float32)
            acc_scr[...] = jnp.zeros(acc_scr.shape, jnp.float32)

        def scores_of(k_ref, causal):
            s_t = jnp.dot(k_ref[...], q_scr[...], preferred_element_type=jnp.float32) * score_scale
            if causal:
                key = lax.broadcasted_iota(jnp.int32, (BLOCK, rows), 0)
                tok = lax.broadcasted_iota(jnp.int32, (BLOCK, rows), 1) % tok_rows
                s_t = jnp.where(key <= tok, s_t, -1e30)
            return s_t

        def step(first_causal, with_second):
            parts = [(scores_of(ka_ref, first_causal), va_ref)]
            if with_second:
                parts.append((scores_of(kb_ref, False), vb_ref))
            m_old = m_scr[...]
            m_new = m_old
            for s_t, _ in parts:
                m_new = jnp.maximum(m_new, jnp.max(s_t, axis=0, keepdims=True))
            factor = jnp.exp(m_old - m_new)
            l_new = l_scr[...] * factor
            acc_new = acc_scr[...] * factor
            for s_t, ref in parts:
                expo = jnp.exp(s_t - m_new)
                l_new = l_new + jnp.sum(expo, axis=0, keepdims=True)
                acc_new = acc_new + jnp.dot(ref[...], expo.astype(jnp.bfloat16), preferred_element_type=jnp.float32)
            l_scr[...] = l_new
            acc_scr[...] = acc_new
            m_scr[...] = m_new

        n = count_ref[0]
        second = 2 * i + 1 < n

        @pl.when((i == 0) & second)
        def _():
            step(True, True)

        @pl.when((i == 0) & jnp.logical_not(second))
        def _():
            step(True, False)

        @pl.when((i > 0) & second)
        def _():
            step(False, True)

        @pl.when((i > 0) & (2 * i < n) & jnp.logical_not(second))
        def _():
            step(False, False)

        @pl.when(i == steps - 1)
        def _():
            for h in range(head_count):
                cols = slice(h * tok_rows, (h + 1) * tok_rows)
                result = acc_scr[:, cols] / l_scr[:, cols]
                o_ref[:, h * HD:(h + 1) * HD] = result.T.astype(o_ref.dtype)

    grid_spec = pltpu.PrefetchScalarGridSpec(
        num_scalar_prefetch=2,
        grid=(steps,),
        in_specs=[
            pl.BlockSpec((tok_rows, head_count * HD), lambda i, o, c: (0, 0)),
            pl.BlockSpec((BLOCK, HD), lambda i, o, c: (o[0, 2 * i], 0)),
            pl.BlockSpec((BLOCK, HD), lambda i, o, c: (o[0, 2 * i + 1], 0)),
            pl.BlockSpec((HD, BLOCK), lambda i, o, c: (o[1, 2 * i], 0)),
            pl.BlockSpec((HD, BLOCK), lambda i, o, c: (o[1, 2 * i + 1], 0)),
        ],
        out_specs=pl.BlockSpec((tok_rows, head_count * HD), lambda i, o, c: (0, 0)),
        scratch_shapes=[
            pltpu.VMEM((HD, rows), jnp.bfloat16),
            pltpu.VMEM((1, rows), jnp.float32),
            pltpu.VMEM((1, rows), jnp.float32),
            pltpu.VMEM((HD, rows), jnp.float32),
        ],
    )
    return pl.pallas_call(
        kernel,
        grid_spec=grid_spec,
        out_shape=jax.ShapeDtypeStruct((tok_rows, head_count * HD), jnp.bfloat16),
        compiler_params=pltpu.CompilerParams(dimension_semantics=("arbitrary",)),
    )(order_physical, count, queries, key_all, key_all, value_all, value_all)


def solution(mesh):
    n_fsdp, n_seq = mesh.devices.shape
    n_c = 2
    n_zh = n_fsdp // n_c
    n_zl = 2
    n_y = 8
    n_x = n_seq // (n_zl * n_y)
    fine = Mesh(mesh.devices.reshape(n_zh, n_c, n_zl, n_x, n_y), FSDP_AXES + SEQ_AXES)
    tok = P(SEQ_AXES, FSDP_AXES)
    return jax.shard_map(
        shards,
        mesh=fine,
        in_specs=(tok, tok, P(FSDP_AXES, None), P(), P(), P()),
        out_specs=tok,
        check_vma=False,
    )
```

```python
import math

import jax
import jax.numpy as jnp
import numpy as np
from jax import lax
from jax.experimental import pallas as pl
from jax.experimental.pallas import tpu as pltpu
from jax.sharding import Mesh
from jax.sharding import PartitionSpec as P

HD = 128
BLOCK = 128
FSDP_AXES = ("zh", "c")
SEQ_AXES = ("zl", "x", "y")


def ancestry_table(parents, slot_block):
    block_count = parents.shape[0]
    block_ids = jnp.arange(block_count, dtype=jnp.int32)
    linked = (parents[:, None] == block_ids[None, :]).astype(jnp.float32)
    ancestry = jnp.maximum(jnp.eye(block_count, dtype=jnp.float32), linked)
    for sweep in range(block_count.bit_length()):
        ancestry = jnp.minimum(jnp.dot(ancestry, ancestry, precision=lax.Precision.HIGHEST), 1.0)
    placement = (slot_block[:, None] == block_ids[None, :]).astype(jnp.float32)
    first_pass = jnp.dot(placement, ancestry, precision=lax.Precision.HIGHEST)
    return jnp.dot(first_pass, placement.T, precision=lax.Precision.HIGHEST)


def seq_index():
    return (lax.axis_index("zl") * lax.axis_size("x") + lax.axis_index("x")) * lax.axis_size("y") + lax.axis_index("y")


def fsdp_index():
    return lax.axis_index("zh") * lax.axis_size("c") + lax.axis_index("c")


def shards(hidden, queries, kv_weight, kv_bias, parents, slot_block):
    tok_rows = hidden.shape[0]
    per_device = tok_rows // BLOCK
    head_count = queries.shape[1] // HD
    score_scale = 1.0 / math.sqrt(HD)
    f_index = fsdp_index()
    n_zh = lax.axis_size("zh")
    n_c = lax.axis_size("c")
    cols = kv_weight.shape[1]
    per_head = cols // (n_zh * n_c)
    partial_sums = jnp.dot(hidden, kv_weight, preferred_element_type=jnp.float32)
    partial_sums = partial_sums.reshape(tok_rows, n_zh, n_c, per_head).transpose(2, 1, 0, 3)
    from_core = lax.all_to_all(partial_sums, "c", 0, 0)
    core_sums = jnp.sum(from_core, axis=0)
    from_chip = lax.all_to_all(core_sums, "zh", 0, 0)
    head_cols = jnp.sum(from_chip, axis=0)
    head_bias = lax.dynamic_slice_in_dim(kv_bias, f_index * 2 * HD, 2 * HD, 0)
    both_parts = (head_cols + head_bias).astype(jnp.bfloat16)
    kv_block = jnp.concatenate([both_parts[:, :HD], both_parts[:, HD:].T], axis=0)
    visible = ancestry_table(parents, slot_block)
    own_slot = seq_index() * per_device
    own_visible = lax.dynamic_slice_in_dim(visible, own_slot, per_device, 0)
    n_zl, n_x, n_y = lax.axis_size("zl"), lax.axis_size("x"), lax.axis_size("y")
    plane_size = n_zl * n_y
    values_t = both_parts[:, HD:].T
    split = HD // 2
    part_a = jnp.concatenate([both_parts[:, :HD], values_t[:split]], axis=0)
    part_b = values_t[split:]
    plane_a = lax.all_to_all(jnp.broadcast_to(part_a[None], (plane_size,) + part_a.shape), ("zl", "y"), 0, 0)
    key_all = lax.all_gather(plane_a, "x", axis=0, tiled=True).reshape(-1, HD)
    row_b = lax.all_gather(part_b[None], "x", axis=0, tiled=True)
    value_all = lax.all_to_all(
        jnp.broadcast_to(row_b[None], (plane_size,) + row_b.shape), ("zl", "y"), 0, 0
    ).reshape(-1, HD)
    slots = jnp.arange(visible.shape[1], dtype=jnp.int32)
    slot_zl = slots // (n_x * n_y)
    slot_x = (slots // n_y) % n_x
    slot_y = slots % n_y
    key_physical = (slot_x * n_zl + slot_zl) * n_y + slot_y
    value_physical = (slot_zl * n_y + slot_y) * n_x + slot_x
    others = (own_visible[0] > 0.5) & (slots != own_slot)
    count = jnp.sum(others.astype(jnp.int32)) + 1
    position = jnp.cumsum(others.astype(jnp.int32))
    wanted = jnp.minimum(slots, count - 1)
    hit = others[None, :] & (position[None, :] == wanted[:, None])
    order = jnp.where(wanted == 0, own_slot, jnp.sum(jnp.where(hit, slots[None, :], 0), axis=1))
    order_physical = jnp.stack([key_physical[order], value_physical[order]]).astype(jnp.int32)
    return attention(order_physical, count.reshape(1), queries, key_all, value_all, head_count, score_scale)


def attention(order_physical, count, queries, key_all, value_all, head_count, score_scale):
    tok_rows = queries.shape[0]
    rows = tok_rows * head_count
    steps = order_physical.shape[1] // 2

    split = HD // 2

    def kernel(order_ref, count_ref, q_ref, ka_ref, kb_ref, va_ref, vb_ref, o_ref, q_scr, m_scr, l_scr, acc_scr):
        i = pl.program_id(0)

        @pl.when(i == 0)
        def _():
            for h in range(head_count):
                q_h = q_ref[:, h * HD:(h + 1) * HD].astype(jnp.float32)
                q_scr[:, h * tok_rows:(h + 1) * tok_rows] = q_h.T.astype(jnp.bfloat16)
            m_scr[...] = jnp.full(m_scr.shape, -1e30, jnp.float32)
            l_scr[...] = jnp.zeros(l_scr.shape, jnp.float32)
            acc_scr[...] = jnp.zeros(acc_scr.shape, jnp.float32)

        def scores_of(k_ref, causal):
            s_t = jnp.dot(k_ref[:BLOCK, :], q_scr[...], preferred_element_type=jnp.float32) * score_scale
            if causal:
                key = lax.broadcasted_iota(jnp.int32, (BLOCK, rows), 0)
                tok = lax.broadcasted_iota(jnp.int32, (BLOCK, rows), 1) % tok_rows
                s_t = jnp.where(key <= tok, s_t, -1e30)
            return s_t

        def step(first_causal, with_second):
            parts = [(scores_of(ka_ref, first_causal), ka_ref, va_ref)]
            if with_second:
                parts.append((scores_of(kb_ref, False), kb_ref, vb_ref))
            m_old = m_scr[...]
            m_new = m_old
            for s_t, _, _ in parts:
                m_new = jnp.maximum(m_new, jnp.max(s_t, axis=0, keepdims=True))
            factor = jnp.exp(m_old - m_new)
            l_new = l_scr[...] * factor
            acc_lo = acc_scr[:split, :] * factor
            acc_hi = acc_scr[split:, :] * factor
            for s_t, k_ref, v_ref in parts:
                expo = jnp.exp(s_t - m_new)
                l_new = l_new + jnp.sum(expo, axis=0, keepdims=True)
                weights = expo.astype(jnp.bfloat16)
                acc_lo = acc_lo + jnp.dot(k_ref[BLOCK:, :], weights, preferred_element_type=jnp.float32)
                acc_hi = acc_hi + jnp.dot(v_ref[...], weights, preferred_element_type=jnp.float32)
            l_scr[...] = l_new
            acc_scr[:split, :] = acc_lo
            acc_scr[split:, :] = acc_hi
            m_scr[...] = m_new

        n = count_ref[0]
        second = 2 * i + 1 < n

        @pl.when((i == 0) & second)
        def _():
            step(True, True)

        @pl.when((i == 0) & jnp.logical_not(second))
        def _():
            step(True, False)

        @pl.when((i > 0) & second)
        def _():
            step(False, True)

        @pl.when((i > 0) & (2 * i < n) & jnp.logical_not(second))
        def _():
            step(False, False)

        @pl.when(i == steps - 1)
        def _():
            for h in range(head_count):
                cols = slice(h * tok_rows, (h + 1) * tok_rows)
                result = acc_scr[:, cols] / l_scr[:, cols]
                o_ref[:, h * HD:(h + 1) * HD] = result.T.astype(o_ref.dtype)

    grid_spec = pltpu.PrefetchScalarGridSpec(
        num_scalar_prefetch=2,
        grid=(steps,),
        in_specs=[
            pl.BlockSpec((tok_rows, head_count * HD), lambda i, o, c: (0, 0)),
            pl.BlockSpec((BLOCK + split, HD), lambda i, o, c: (o[0, 2 * i], 0)),
            pl.BlockSpec((BLOCK + split, HD), lambda i, o, c: (o[0, 2 * i + 1], 0)),
            pl.BlockSpec((HD - split, BLOCK), lambda i, o, c: (o[1, 2 * i], 0)),
            pl.BlockSpec((HD - split, BLOCK), lambda i, o, c: (o[1, 2 * i + 1], 0)),
        ],
        out_specs=pl.BlockSpec((tok_rows, head_count * HD), lambda i, o, c: (0, 0)),
        scratch_shapes=[
            pltpu.VMEM((HD, rows), jnp.bfloat16),
            pltpu.VMEM((1, rows), jnp.float32),
            pltpu.VMEM((1, rows), jnp.float32),
            pltpu.VMEM((HD, rows), jnp.float32),
        ],
    )
    return pl.pallas_call(
        kernel,
        grid_spec=grid_spec,
        out_shape=jax.ShapeDtypeStruct((tok_rows, head_count * HD), jnp.bfloat16),
        compiler_params=pltpu.CompilerParams(dimension_semantics=("arbitrary",)),
    )(order_physical, count, queries, key_all, key_all, value_all, value_all)


def solution(mesh):
    n_fsdp, n_seq = mesh.devices.shape
    n_c = 2
    n_zh = n_fsdp // n_c
    n_zl = 2
    n_y = 8
    n_x = n_seq // (n_zl * n_y)
    fine = Mesh(mesh.devices.reshape(n_zh, n_c, n_zl, n_x, n_y), FSDP_AXES + SEQ_AXES)
    tok = P(SEQ_AXES, FSDP_AXES)
    return jax.shard_map(
        shards,
        mesh=fine,
        in_specs=(tok, tok, P(FSDP_AXES, None), P(), P(), P()),
        out_specs=tok,
        check_vma=False,
    )
```

```python
import math

import jax
import jax.numpy as jnp
import numpy as np
from jax import lax
from jax.experimental import pallas as pl
from jax.experimental.pallas import tpu as pltpu
from jax.sharding import Mesh
from jax.sharding import PartitionSpec as P

HD = 128
BLOCK = 128
FSDP_AXES = ("zh", "c")
SEQ_AXES = ("zl", "x", "y")
SLOTS_PER_STEP = 4


def ancestry_table(parents, slot_block):
    block_count = parents.shape[0]
    block_ids = jnp.arange(block_count, dtype=jnp.int32)
    linked = (parents[:, None] == block_ids[None, :]).astype(jnp.float32)
    ancestry = jnp.maximum(jnp.eye(block_count, dtype=jnp.float32), linked)
    for sweep in range(block_count.bit_length()):
        ancestry = jnp.minimum(jnp.dot(ancestry, ancestry, precision=lax.Precision.HIGHEST), 1.0)
    placement = (slot_block[:, None] == block_ids[None, :]).astype(jnp.float32)
    first_pass = jnp.dot(placement, ancestry, precision=lax.Precision.HIGHEST)
    return jnp.dot(first_pass, placement.T, precision=lax.Precision.HIGHEST)


def seq_index():
    return (lax.axis_index("zl") * lax.axis_size("x") + lax.axis_index("x")) * lax.axis_size("y") + lax.axis_index("y")


def fsdp_index():
    return lax.axis_index("zh") * lax.axis_size("c") + lax.axis_index("c")


def shards(hidden, queries, kv_weight, kv_bias, parents, slot_block):
    tok_rows = hidden.shape[0]
    per_device = tok_rows // BLOCK
    head_count = queries.shape[1] // HD
    score_scale = 1.0 / math.sqrt(HD)
    f_index = fsdp_index()
    n_zh = lax.axis_size("zh")
    n_c = lax.axis_size("c")
    cols = kv_weight.shape[1]
    per_head = cols // (n_zh * n_c)
    partial_sums = jnp.dot(hidden, kv_weight, preferred_element_type=jnp.float32)
    partial_sums = partial_sums.reshape(tok_rows, n_zh, n_c, per_head).transpose(2, 1, 0, 3)
    from_core = lax.all_to_all(partial_sums, "c", 0, 0)
    core_sums = jnp.sum(from_core, axis=0)
    from_chip = lax.all_to_all(core_sums, "zh", 0, 0)
    head_cols = jnp.sum(from_chip, axis=0)
    head_bias = lax.dynamic_slice_in_dim(kv_bias, f_index * 2 * HD, 2 * HD, 0)
    both_parts = (head_cols + head_bias).astype(jnp.bfloat16)
    kv_block = jnp.concatenate([both_parts[:, :HD], both_parts[:, HD:].T], axis=0)
    visible = ancestry_table(parents, slot_block)
    own_slot = seq_index() * per_device
    own_visible = lax.dynamic_slice_in_dim(visible, own_slot, per_device, 0)
    n_zl, n_x, n_y = lax.axis_size("zl"), lax.axis_size("x"), lax.axis_size("y")
    plane_size = n_zl * n_y
    values_t = both_parts[:, HD:].T
    split = HD // 2
    part_a = jnp.concatenate([both_parts[:, :HD], values_t[:split]], axis=0)
    part_b = values_t[split:]
    plane_a = lax.all_to_all(jnp.broadcast_to(part_a[None], (plane_size,) + part_a.shape), ("zl", "y"), 0, 0)
    key_all = lax.all_gather(plane_a, "x", axis=0, tiled=True).reshape(-1, HD)
    row_b = lax.all_gather(part_b[None], "x", axis=0, tiled=True)
    value_all = lax.all_to_all(
        jnp.broadcast_to(row_b[None], (plane_size,) + row_b.shape), ("zl", "y"), 0, 0
    ).reshape(-1, HD)
    slots = jnp.arange(visible.shape[1], dtype=jnp.int32)
    slot_zl = slots // (n_x * n_y)
    slot_x = (slots // n_y) % n_x
    slot_y = slots % n_y
    key_physical = (slot_x * n_zl + slot_zl) * n_y + slot_y
    value_physical = (slot_zl * n_y + slot_y) * n_x + slot_x
    others = (own_visible[0] > 0.5) & (slots != own_slot)
    count = jnp.sum(others.astype(jnp.int32)) + 1
    position = jnp.cumsum(others.astype(jnp.int32))
    wanted = jnp.minimum(slots, count - 1)
    hit = others[None, :] & (position[None, :] == wanted[:, None])
    order = jnp.where(wanted == 0, own_slot, jnp.sum(jnp.where(hit, slots[None, :], 0), axis=1))
    order_physical = jnp.stack([key_physical[order], value_physical[order]]).astype(jnp.int32)
    return attention(order_physical, count.reshape(1), queries, key_all, value_all, head_count, score_scale)


def attention(order_physical, count, queries, key_all, value_all, head_count, score_scale):
    tok_rows = queries.shape[0]
    rows = tok_rows * head_count
    group = SLOTS_PER_STEP
    steps = order_physical.shape[1] // group
    split = HD // 2

    def kernel(order_ref, count_ref, q_ref, *refs):
        k_refs = refs[:group]
        v_refs = refs[group:2 * group]
        o_ref, q_scr, m_scr, l_scr, acc_scr = refs[2 * group:]
        i = pl.program_id(0)

        @pl.when(i == 0)
        def _():
            for h in range(head_count):
                q_h = q_ref[:, h * HD:(h + 1) * HD].astype(jnp.float32)
                q_scr[:, h * tok_rows:(h + 1) * tok_rows] = q_h.T.astype(jnp.bfloat16)
            m_scr[...] = jnp.full(m_scr.shape, -1e30, jnp.float32)
            l_scr[...] = jnp.zeros(l_scr.shape, jnp.float32)
            acc_scr[...] = jnp.zeros(acc_scr.shape, jnp.float32)

        def scores_of(k_ref, causal):
            s_t = jnp.dot(k_ref[:BLOCK, :], q_scr[...], preferred_element_type=jnp.float32) * score_scale
            if causal:
                key = lax.broadcasted_iota(jnp.int32, (BLOCK, rows), 0)
                tok = lax.broadcasted_iota(jnp.int32, (BLOCK, rows), 1) % tok_rows
                s_t = jnp.where(key <= tok, s_t, -1e30)
            return s_t

        def step(first_causal, valid):
            parts = [
                (scores_of(k_refs[g], first_causal and g == 0), k_refs[g], v_refs[g]) for g in range(valid)
            ]
            m_old = m_scr[...]
            m_new = m_old
            for s_t, _, _ in parts:
                m_new = jnp.maximum(m_new, jnp.max(s_t, axis=0, keepdims=True))
            factor = jnp.exp(m_old - m_new)
            l_new = l_scr[...] * factor
            acc_lo = acc_scr[:split, :] * factor
            acc_hi = acc_scr[split:, :] * factor
            for s_t, k_ref, v_ref in parts:
                expo = jnp.exp(s_t - m_new)
                l_new = l_new + jnp.sum(expo, axis=0, keepdims=True)
                weights = expo.astype(jnp.bfloat16)
                acc_lo = acc_lo + jnp.dot(k_ref[BLOCK:, :], weights, preferred_element_type=jnp.float32)
                acc_hi = acc_hi + jnp.dot(v_ref[...], weights, preferred_element_type=jnp.float32)
            l_scr[...] = l_new
            acc_scr[:split, :] = acc_lo
            acc_scr[split:, :] = acc_hi
            m_scr[...] = m_new

        left = count_ref[0] - group * i
        for first in (True, False):
            for valid in range(1, group + 1):
                at_valid = (left >= valid) if valid == group else (left == valid)
                at_step = (i == 0) if first else (i > 0)

                @pl.when(at_step & at_valid)
                def _(first=first, valid=valid):
                    step(first, valid)

        @pl.when(i == steps - 1)
        def _():
            for h in range(head_count):
                cols = slice(h * tok_rows, (h + 1) * tok_rows)
                result = acc_scr[:, cols] / l_scr[:, cols]
                o_ref[:, h * HD:(h + 1) * HD] = result.T.astype(o_ref.dtype)

    def key_map(g):
        return lambda i, o, c: (o[0, group * i + g], 0)

    def value_map(g):
        return lambda i, o, c: (o[1, group * i + g], 0)

    grid_spec = pltpu.PrefetchScalarGridSpec(
        num_scalar_prefetch=2,
        grid=(steps,),
        in_specs=[pl.BlockSpec((tok_rows, head_count * HD), lambda i, o, c: (0, 0))]
        + [pl.BlockSpec((BLOCK + split, HD), key_map(g)) for g in range(group)]
        + [pl.BlockSpec((HD - split, BLOCK), value_map(g)) for g in range(group)],
        out_specs=pl.BlockSpec((tok_rows, head_count * HD), lambda i, o, c: (0, 0)),
        scratch_shapes=[
            pltpu.VMEM((HD, rows), jnp.bfloat16),
            pltpu.VMEM((1, rows), jnp.float32),
            pltpu.VMEM((1, rows), jnp.float32),
            pltpu.VMEM((HD, rows), jnp.float32),
        ],
    )
    return pl.pallas_call(
        kernel,
        grid_spec=grid_spec,
        out_shape=jax.ShapeDtypeStruct((tok_rows, head_count * HD), jnp.bfloat16),
        compiler_params=pltpu.CompilerParams(dimension_semantics=("arbitrary",)),
    )(order_physical, count, queries, *([key_all] * group), *([value_all] * group))


def solution(mesh):
    n_fsdp, n_seq = mesh.devices.shape
    n_c = 2
    n_zh = n_fsdp // n_c
    n_zl = 2
    n_y = 8
    n_x = n_seq // (n_zl * n_y)
    fine = Mesh(mesh.devices.reshape(n_zh, n_c, n_zl, n_x, n_y), FSDP_AXES + SEQ_AXES)
    tok = P(SEQ_AXES, FSDP_AXES)
    return jax.shard_map(
        shards,
        mesh=fine,
        in_specs=(tok, tok, P(FSDP_AXES, None), P(), P(), P()),
        out_specs=tok,
        check_vma=False,
    )
```

```python
import math

import jax
import jax.numpy as jnp
import numpy as np
from jax import lax
from jax.experimental import pallas as pl
from jax.experimental.pallas import tpu as pltpu
from jax.sharding import Mesh
from jax.sharding import PartitionSpec as P

HD = 128
BLOCK = 128
FSDP_AXES = ("zh", "c")
SEQ_AXES = ("zl", "x", "y")
SLOTS_PER_STEP = 8


def ancestry_table(parents, slot_block):
    block_count = parents.shape[0]
    block_ids = jnp.arange(block_count, dtype=jnp.int32)
    linked = (parents[:, None] == block_ids[None, :]).astype(jnp.float32)
    ancestry = jnp.maximum(jnp.eye(block_count, dtype=jnp.float32), linked)
    for sweep in range(block_count.bit_length()):
        ancestry = jnp.minimum(jnp.dot(ancestry, ancestry, precision=lax.Precision.HIGHEST), 1.0)
    placement = (slot_block[:, None] == block_ids[None, :]).astype(jnp.float32)
    first_pass = jnp.dot(placement, ancestry, precision=lax.Precision.HIGHEST)
    return jnp.dot(first_pass, placement.T, precision=lax.Precision.HIGHEST)


def seq_index():
    return (lax.axis_index("zl") * lax.axis_size("x") + lax.axis_index("x")) * lax.axis_size("y") + lax.axis_index("y")


def fsdp_index():
    return lax.axis_index("zh") * lax.axis_size("c") + lax.axis_index("c")


def shards(hidden, queries, kv_weight, kv_bias, parents, slot_block):
    tok_rows = hidden.shape[0]
    per_device = tok_rows // BLOCK
    head_count = queries.shape[1] // HD
    score_scale = 1.0 / math.sqrt(HD)
    f_index = fsdp_index()
    n_zh = lax.axis_size("zh")
    n_c = lax.axis_size("c")
    cols = kv_weight.shape[1]
    per_head = cols // (n_zh * n_c)
    partial_sums = jnp.dot(hidden, kv_weight, preferred_element_type=jnp.float32)
    partial_sums = partial_sums.reshape(tok_rows, n_zh, n_c, per_head).transpose(2, 1, 0, 3)
    from_core = lax.all_to_all(partial_sums, "c", 0, 0)
    core_sums = jnp.sum(from_core, axis=0)
    from_chip = lax.all_to_all(core_sums, "zh", 0, 0)
    head_cols = jnp.sum(from_chip, axis=0)
    head_bias = lax.dynamic_slice_in_dim(kv_bias, f_index * 2 * HD, 2 * HD, 0)
    both_parts = (head_cols + head_bias).astype(jnp.bfloat16)
    kv_block = jnp.concatenate([both_parts[:, :HD], both_parts[:, HD:].T], axis=0)
    visible = ancestry_table(parents, slot_block)
    own_slot = seq_index() * per_device
    own_visible = lax.dynamic_slice_in_dim(visible, own_slot, per_device, 0)
    n_zl, n_x, n_y = lax.axis_size("zl"), lax.axis_size("x"), lax.axis_size("y")
    plane_size = n_zl * n_y
    values_t = both_parts[:, HD:].T
    split = HD // 2
    part_a = jnp.concatenate([both_parts[:, :HD], values_t[:split]], axis=0)
    part_b = values_t[split:]
    plane_a = lax.all_to_all(jnp.broadcast_to(part_a[None], (plane_size,) + part_a.shape), ("zl", "y"), 0, 0)
    key_all = lax.all_gather(plane_a, "x", axis=0, tiled=True).reshape(-1, HD)
    row_b = lax.all_gather(part_b[None], "x", axis=0, tiled=True)
    value_all = lax.all_to_all(
        jnp.broadcast_to(row_b[None], (plane_size,) + row_b.shape), ("zl", "y"), 0, 0
    ).reshape(-1, HD)
    slots = jnp.arange(visible.shape[1], dtype=jnp.int32)
    slot_zl = slots // (n_x * n_y)
    slot_x = (slots // n_y) % n_x
    slot_y = slots % n_y
    key_physical = (slot_x * n_zl + slot_zl) * n_y + slot_y
    value_physical = (slot_zl * n_y + slot_y) * n_x + slot_x
    others = (own_visible[0] > 0.5) & (slots != own_slot)
    count = jnp.sum(others.astype(jnp.int32)) + 1
    position = jnp.cumsum(others.astype(jnp.int32))
    wanted = jnp.minimum(slots, count - 1)
    hit = others[None, :] & (position[None, :] == wanted[:, None])
    order = jnp.where(wanted == 0, own_slot, jnp.sum(jnp.where(hit, slots[None, :], 0), axis=1))
    order_physical = jnp.stack([key_physical[order], value_physical[order]]).astype(jnp.int32)
    return attention(order_physical, count.reshape(1), queries, key_all, value_all, head_count, score_scale)


def attention(order_physical, count, queries, key_all, value_all, head_count, score_scale):
    tok_rows = queries.shape[0]
    rows = tok_rows * head_count
    group = SLOTS_PER_STEP
    steps = order_physical.shape[1] // group
    split = HD // 2

    def kernel(order_ref, count_ref, q_ref, *refs):
        k_refs = refs[:group]
        v_refs = refs[group:2 * group]
        o_ref, q_scr, m_scr, l_scr, acc_scr = refs[2 * group:]
        i = pl.program_id(0)

        @pl.when(i == 0)
        def _():
            for h in range(head_count):
                q_h = q_ref[:, h * HD:(h + 1) * HD].astype(jnp.float32)
                q_scr[:, h * tok_rows:(h + 1) * tok_rows] = q_h.T.astype(jnp.bfloat16)
            m_scr[...] = jnp.full(m_scr.shape, -1e30, jnp.float32)
            l_scr[...] = jnp.zeros(l_scr.shape, jnp.float32)
            acc_scr[...] = jnp.zeros(acc_scr.shape, jnp.float32)

        def scores_of(k_ref, causal):
            s_t = jnp.dot(k_ref[:BLOCK, :], q_scr[...], preferred_element_type=jnp.float32) * score_scale
            if causal:
                key = lax.broadcasted_iota(jnp.int32, (BLOCK, rows), 0)
                tok = lax.broadcasted_iota(jnp.int32, (BLOCK, rows), 1) % tok_rows
                s_t = jnp.where(key <= tok, s_t, -1e30)
            return s_t

        def step(first_causal, valid):
            parts = [
                (scores_of(k_refs[g], first_causal and g == 0), k_refs[g], v_refs[g]) for g in range(valid)
            ]
            m_old = m_scr[...]
            m_new = m_old
            for s_t, _, _ in parts:
                m_new = jnp.maximum(m_new, jnp.max(s_t, axis=0, keepdims=True))
            factor = jnp.exp(m_old - m_new)
            l_new = l_scr[...] * factor
            acc_lo = acc_scr[:split, :] * factor
            acc_hi = acc_scr[split:, :] * factor
            for s_t, k_ref, v_ref in parts:
                expo = jnp.exp(s_t - m_new)
                l_new = l_new + jnp.sum(expo, axis=0, keepdims=True)
                weights = expo.astype(jnp.bfloat16)
                acc_lo = acc_lo + jnp.dot(k_ref[BLOCK:, :], weights, preferred_element_type=jnp.float32)
                acc_hi = acc_hi + jnp.dot(v_ref[...], weights, preferred_element_type=jnp.float32)
            l_scr[...] = l_new
            acc_scr[:split, :] = acc_lo
            acc_scr[split:, :] = acc_hi
            m_scr[...] = m_new

        left = count_ref[0] - group * i
        for first in (True, False):
            for valid in range(1, group + 1):
                at_valid = (left >= valid) if valid == group else (left == valid)
                at_step = (i == 0) if first else (i > 0)

                @pl.when(at_step & at_valid)
                def _(first=first, valid=valid):
                    step(first, valid)

        @pl.when(i == steps - 1)
        def _():
            for h in range(head_count):
                cols = slice(h * tok_rows, (h + 1) * tok_rows)
                result = acc_scr[:, cols] / l_scr[:, cols]
                o_ref[:, h * HD:(h + 1) * HD] = result.T.astype(o_ref.dtype)

    def key_map(g):
        return lambda i, o, c: (o[0, group * i + g], 0)

    def value_map(g):
        return lambda i, o, c: (o[1, group * i + g], 0)

    grid_spec = pltpu.PrefetchScalarGridSpec(
        num_scalar_prefetch=2,
        grid=(steps,),
        in_specs=[pl.BlockSpec((tok_rows, head_count * HD), lambda i, o, c: (0, 0))]
        + [pl.BlockSpec((BLOCK + split, HD), key_map(g)) for g in range(group)]
        + [pl.BlockSpec((HD - split, BLOCK), value_map(g)) for g in range(group)],
        out_specs=pl.BlockSpec((tok_rows, head_count * HD), lambda i, o, c: (0, 0)),
        scratch_shapes=[
            pltpu.VMEM((HD, rows), jnp.bfloat16),
            pltpu.VMEM((1, rows), jnp.float32),
            pltpu.VMEM((1, rows), jnp.float32),
            pltpu.VMEM((HD, rows), jnp.float32),
        ],
    )
    return pl.pallas_call(
        kernel,
        grid_spec=grid_spec,
        out_shape=jax.ShapeDtypeStruct((tok_rows, head_count * HD), jnp.bfloat16),
        compiler_params=pltpu.CompilerParams(dimension_semantics=("arbitrary",)),
    )(order_physical, count, queries, *([key_all] * group), *([value_all] * group))


def solution(mesh):
    n_fsdp, n_seq = mesh.devices.shape
    n_c = 2
    n_zh = n_fsdp // n_c
    n_zl = 2
    n_y = 8
    n_x = n_seq // (n_zl * n_y)
    fine = Mesh(mesh.devices.reshape(n_zh, n_c, n_zl, n_x, n_y), FSDP_AXES + SEQ_AXES)
    tok = P(SEQ_AXES, FSDP_AXES)
    return jax.shard_map(
        shards,
        mesh=fine,
        in_specs=(tok, tok, P(FSDP_AXES, None), P(), P(), P()),
        out_specs=tok,
        check_vma=False,
    )
```
